32 devices in a mesh: gx: 8 (over z, x), gy: 4 (over y, core).
Axes of the slice: x: 2, y: 2, z: 4, core: 2. Of those that a mesh axis runs over, the one named last changes fastest.
Arguments:
- modes_x: float32 [32, 131072], P(None, ('gx', 'gy')), may hold values from -6 to 6
- previous_p: float32 [32, 131072], P(None, ('gx', 'gy')), may hold values from -6 to 6
- stiff_blocks: float32 [1024, 4, 128, 128], P(('gx', 'gy'))
- mass_blocks: float32 [1024, 4, 128, 128], P(('gx', 'gy'))
- block_pattern: int32 [1024, 4], P(('gx', 'gy')), may hold values from 0 to 35, as said below
- lumped_mass: float32 [131072], P(('gx', 'gy')), may hold values from 0.5 to 2
- edge_ends: int32 [2, 131072], P(None, ('gx', 'gy')), may hold values from 0 to 1535, as said below
- ghost_slot: int32 [16384], P(('gx', 'gy')), may hold values from 0 to 1023, as said below
- owner_node: int32 [32768], P(('gx', 'gy')), may hold values from 0 to 1024, as said below
Outputs:
- projected: float32 [32, 131072], P(None, ('gx', 'gy'))
- reduced: float32 [96, 96], replicated
The draws below stay inside these ranges and needn't reach their ends.
Inputs may be any that keep to these rules, and one draw needn't show every extreme that they name: block_pattern[t, r, 0] is r; the other entries name any of the tile's own blocks (below 32) or one of the four received blocks, in the order of the extended vector. `edge_ends`: the two ends of an edge are different entries of its tile's table of 1536; every entry of every table is the tail of some edge of that tile. `ghost_slot`: the entries of one tile are distinct; a ghost on one of the tile's four faces is owned by the tile beside it across that face, or across the opposite face where that tile does not exist; the direction named always has a tile; a tile on the edge of the grid fills all 256 slots of the direction to its inner neighbour. `owner_node`: consistent with ghost_slot: entry (p, d * 256 + c) names the owned node of tile p for which the tile s that sees p in direction d uses slot d * 256 + c, and is 1024 where no such slot is used.
All inputs are finite; a program needn't handle non-finite values.
Results may differ from the reference program's by a relative error of at most 0.000096.
Values sent between devices are 32-bit elements; how exact they have to be, the bound alone decides.
No kernel may reach another device: no remote copies, remote signals or barrier semaphores. Data moves between devices by JAX's collectives and lax.ppermute only.
A program may use at most 128 MiB of HBM per device.

```python
import math
import jax
import jax.numpy as jnp
from jax import lax

MODES = 32
EDGE_DEV = 4096
BLOCK = 128
PER_ROW = 4
SWEEPS = 4
GHOST_FACE = 128
NODE_DEV = 1024
SLOTS = 256
GHOSTS = 512
TABLE = 1536
ROW_BLOCKS = 32
ALL_BLOCKS = 1024
EDGES = 131072
N_GX = 8
N_GY = 4


def operator_blocks(key, low, high, spread):
    key_diag, key_noise = jax.random.split(key)
    shape = (ALL_BLOCKS, PER_ROW, BLOCK, BLOCK)
    diag_vals = jax.random.uniform(key_diag, (ALL_BLOCKS, BLOCK), jnp.float32, low, high)
    noise = jax.random.normal(key_noise, shape, jnp.float32) * spread
    first = (jnp.arange(PER_ROW) == 0).astype(jnp.float32)
    eye = jnp.eye(BLOCK, dtype=jnp.float32)
    return noise + first[None, :, None, None] * eye[None, None] * diag_vals[:, None, :, None]


def draw_stiff_blocks(key, part):
    return operator_blocks(jax.random.fold_in(key, 11), 2.0, 6.0, 0.02)


def draw_mass_blocks(key, part):
    return operator_blocks(jax.random.fold_in(key, 12), 1.0, 3.0, 0.01)


def draw_block_pattern(key, part):
    own = (jnp.arange(ALL_BLOCKS, dtype=jnp.int32) % ROW_BLOCKS)[:, None]
    others = jax.random.randint(jax.random.fold_in(key, 13), (ALL_BLOCKS, PER_ROW - 1), 0, ROW_BLOCKS + 4, dtype=jnp.int32)
    return jnp.concatenate([own, others], axis=1)


def draw_edge_ends(key, part):
    devices = N_GX * N_GY

    def one_tile(tile_key):
        key_perm, key_tail, key_head = jax.random.split(tile_key, 3)
        order = jax.random.permutation(key_perm, EDGE_DEV)
        tail = jax.random.randint(key_tail, (EDGE_DEV,), 0, TABLE, dtype=jnp.int32)
        tail = tail.at[order[:TABLE]].set(jnp.arange(TABLE, dtype=jnp.int32))
        head = (tail + 1 + jax.random.randint(key_head, (EDGE_DEV,), 0, TABLE - 1, dtype=jnp.int32)) % TABLE
        return jnp.stack([tail, head])
    tile_keys = jax.random.split(jax.random.fold_in(key, 14), devices)
    stacked = jax.vmap(one_tile)(tile_keys)
    return stacked.transpose(1, 0, 2).reshape(2, devices * EDGE_DEV)


def ghost_links(key):
    devices = N_GX * N_GY
    index = jnp.arange(devices, dtype=jnp.int32)
    row = (index // N_GY)[:, None]
    column = (index % N_GY)[:, None]
    ghost = jnp.arange(GHOSTS, dtype=jnp.int32)
    side = (ghost // GHOST_FACE)[None, :]
    face_keys = jax.random.split(jax.random.fold_in(key, 16), devices * 4)
    shuffled = jax.vmap(lambda one_key: jax.random.permutation(one_key, GHOST_FACE))(face_keys)
    within = shuffled.reshape(devices, GHOSTS).astype(jnp.int32)
    direction = jnp.where(side == 0, jnp.where(row - 1 < 0, 1, 0), jnp.where(side == 1, jnp.where(row + 1 >= N_GX, 0, 1), jnp.where(side == 2, jnp.where(column - 1 < 0, 3, 2), jnp.where(column + 1 >= N_GY, 2, 3))))
    step_x = jnp.where(direction == 0, -1, jnp.where(direction == 1, 1, 0))
    step_y = jnp.where(direction == 2, -1, jnp.where(direction == 3, 1, 0))
    owner = (row + step_x) * N_GY + (column + step_y)
    slot = side % 2 * GHOST_FACE + within
    node = jax.random.randint(jax.random.fold_in(key, 15), (devices, GHOSTS), 0, NODE_DEV, dtype=jnp.int32)
    send = (direction * SLOTS + slot).astype(jnp.int32)
    recv = jnp.full((devices, 4 * SLOTS), NODE_DEV, jnp.int32).at[owner, send].set(node)
    return (send.reshape(-1), recv.reshape(-1))


def draw_ghost_slot(key, part):
    return ghost_links(key)[0]


def draw_owner_node(key, part):
    return ghost_links(key)[1]


def levels(own_key, shape, cuts, low, top_value):
    def one(axis_at, blocks):
        draws = jax.random.uniform(jax.random.fold_in(jax.random.fold_in(own_key, 6), axis_at), (blocks,), jnp.float32, low / len(cuts), top_value / len(cuts))
        return jnp.repeat(jnp.exp(draws), shape[axis_at] // blocks).reshape((-1,) + (1,) * (len(shape) - axis_at - 1))

    loudness = one(*cuts[0])
    for cut in cuts[1:]:
        loudness = loudness * one(*cut)
    return loudness


def centred(key, extent, scale, most, cuts=(), kind=jnp.bfloat16):
    values = jax.random.normal(key, extent, jnp.float32) * scale
    if len(cuts) > 0:
        values = levels(key, extent, cuts, -0.22, 0.18) * values
    return jnp.clip(values, min=-most, max=most).astype(kind)


def setup_inputs(seed: int = 0) -> dict:
    keys = jax.random.split(jax.random.key(seed), 10)
    modes_x = centred(keys[0], (MODES, EDGES), 1.0, 6.0, ((1, 32),), jnp.float32)
    previous_p = centred(keys[1], (MODES, EDGES), 1.0, 6.0, ((1, 32),), jnp.float32)
    stiff_blocks = draw_stiff_blocks(jax.random.fold_in(keys[9], 71), 0)
    mass_blocks = draw_mass_blocks(jax.random.fold_in(keys[9], 71), 0)
    block_pattern = draw_block_pattern(jax.random.fold_in(keys[9], 71), 0)
    lumped_mass = jnp.clip(jnp.exp(math.log(2.0) - 1.3862944 * jax.random.uniform(keys[5], (EDGES,), jnp.float32) ** levels(keys[5], (EDGES,), ((0, 32),), -0.2, 0.2)), 0.5, 2.0)
    edge_ends = draw_edge_ends(jax.random.fold_in(keys[9], 71), 0)
    ghost_slot = draw_ghost_slot(jax.random.fold_in(keys[9], 71), 0)
    owner_node = draw_owner_node(jax.random.fold_in(keys[9], 71), 0)
    return {"modes_x": modes_x, "previous_p": previous_p, "stiff_blocks": stiff_blocks, "mass_blocks": mass_blocks, "block_pattern": block_pattern, "lumped_mass": lumped_mass, "edge_ends": edge_ends, "ghost_slot": ghost_slot, "owner_node": owner_node}


HIGH = lax.Precision.HIGHEST
OMEGA = 0.6

def shift_grid(array, axis, back):
    length = array.shape[axis]
    blank = jnp.zeros_like(lax.slice_in_dim(array, 0, 1, axis=axis))
    if back:
        return jnp.concatenate([lax.slice_in_dim(array, 1, length, axis=axis), blank], axis=axis)
    return jnp.concatenate([blank, lax.slice_in_dim(array, 0, length - 1, axis=axis)], axis=axis)

def reference(modes_x, previous_p, stiff_blocks, mass_blocks, block_pattern, lumped_mass, edge_ends, ghost_slot, owner_node):
    devices = N_GX * N_GY
    ends = edge_ends.reshape(2, devices, EDGE_DEV)
    slots = ghost_slot.reshape(devices, GHOSTS)
    owners = owner_node.reshape(devices, 4 * SLOTS)
    lumped = lumped_mass.reshape(devices, EDGE_DEV)
    stiff = stiff_blocks.reshape(devices, ROW_BLOCKS, PER_ROW, BLOCK, BLOCK)
    mass = mass_blocks.reshape(devices, ROW_BLOCKS, PER_ROW, BLOCK, BLOCK)
    pattern = block_pattern.reshape(devices, ROW_BLOCKS, PER_ROW)

    def extend(field):
        width = field.shape[0]
        grid = field.reshape(width, N_GX, N_GY, EDGE_DEV)
        blank_x = jnp.zeros((width, 1, N_GY, BLOCK), jnp.float32)
        blank_y = jnp.zeros((width, N_GX, 1, BLOCK), jnp.float32)
        upper_x = grid[..., EDGE_DEV - BLOCK:]
        lower_x = grid[..., :BLOCK]
        upper_y = grid[..., EDGE_DEV - 2 * BLOCK:EDGE_DEV - BLOCK]
        lower_y = grid[..., BLOCK:2 * BLOCK]
        below_x = jnp.concatenate([blank_x, upper_x[:, :-1]], axis=1)
        above_x = jnp.concatenate([lower_x[:, 1:], blank_x], axis=1)
        below_y = jnp.concatenate([blank_y, upper_y[:, :, :-1]], axis=2)
        above_y = jnp.concatenate([lower_y[:, :, 1:], blank_y], axis=2)
        whole = jnp.concatenate([grid, below_x, above_x, below_y, above_y], axis=3)
        return whole.reshape(width, devices, EDGE_DEV + 4 * BLOCK)

    def apply_blocks(blocks, extended):

        def one_tile(blk, pat, ext):
            tiles = ext.reshape(ext.shape[0], -1, BLOCK)
            picked = tiles[:, pat]
            return jnp.einsum('vrkj,rkij->vri', picked, blk, precision=HIGH).reshape(ext.shape[0], -1)
        result = jax.vmap(one_tile, in_axes=(0, 0, 1), out_axes=1)(blocks, pattern, extended)
        return result.reshape(result.shape[0], -1)

    def gradient(table):

        def one_tile(tab, ends_tile):
            return tab[:, ends_tile[1]] - tab[:, ends_tile[0]]
        return jax.vmap(one_tile, in_axes=(1, 1), out_axes=1)(table, ends)

    def divergence(values):

        def one_tile(vals, ends_tile):
            start = jnp.zeros((vals.shape[0], TABLE), jnp.float32)
            return start.at[:, ends_tile[1]].add(vals).at[:, ends_tile[0]].add(-vals)
        return jax.vmap(one_tile, in_axes=(1, 1), out_axes=1)(values, ends)

    def move(sent, toward_owner):
        width = sent.shape[0]
        grid = sent.reshape(width, N_GX, N_GY, 4, SLOTS)
        parts = []
        for direction in range(4):
            axis = 1 if direction < 2 else 2
            back = (direction % 2 == 0) == toward_owner
            parts.append(shift_grid(grid[:, :, :, direction], axis, back))
        return jnp.stack(parts, axis=3).reshape(width, devices, 4 * SLOTS)

    def to_owners(table):
        width = table.shape[0]

        def pack(tab, slot_tile):
            return jnp.zeros((width, 4 * SLOTS), jnp.float32).at[:, slot_tile].set(tab[:, NODE_DEV:])
        received = move(jax.vmap(pack, in_axes=(1, 0), out_axes=1)(table, slots), True)

        def land(recv, own_tile):
            return jnp.zeros((width, NODE_DEV + 1), jnp.float32).at[:, own_tile].add(recv)[:, :NODE_DEV]
        return table[..., :NODE_DEV] + jax.vmap(land, in_axes=(1, 0), out_axes=1)(received, owners)

    def to_ghosts(owned):
        width = owned.shape[0]
        padded = jnp.concatenate([owned, jnp.zeros((width, devices, 1), jnp.float32)], axis=2)

        def pick(pad, own_tile):
            return pad[:, own_tile]
        received = move(jax.vmap(pick, in_axes=(1, 0), out_axes=1)(padded, owners), False)

        def fetch(recv, slot_tile):
            return recv[:, slot_tile]
        ghosts = jax.vmap(fetch, in_axes=(1, 0), out_axes=1)(received, slots)
        return jnp.concatenate([owned, ghosts], axis=2)

    def tiles_of(field):
        return field.reshape(field.shape[0], devices, EDGE_DEV)
    near_x = extend(modes_x)
    stiff_x = apply_blocks(stiff, near_x)
    mass_x = apply_blocks(mass, near_x)
    near_p = extend(previous_p)
    stiff_p = apply_blocks(stiff, near_p)
    mass_p = apply_blocks(mass, near_p)
    ritz = jnp.sum(modes_x * stiff_x, axis=1) / jnp.sum(modes_x * mass_x, axis=1)
    residual = stiff_x - ritz[:, None] * mass_x
    mass_r = apply_blocks(mass, extend(residual))
    rhs = to_owners(divergence(tiles_of(mass_r)))

    def weigh(lump_tile, ends_tile):
        start = jnp.zeros((TABLE,), jnp.float32)
        return start.at[ends_tile[1]].add(lump_tile).at[ends_tile[0]].add(lump_tile)
    weight_table = jax.vmap(weigh, in_axes=(0, 1))(lumped, ends)[None]
    diagonal = to_owners(weight_table)
    potential = OMEGA * rhs / diagonal
    for sweep in range(SWEEPS - 1):
        flux = lumped[None] * gradient(to_ghosts(potential))
        applied = to_owners(divergence(flux))
        potential = potential + OMEGA * (rhs - applied) / diagonal
    projected = residual - gradient(to_ghosts(potential)).reshape(residual.shape[0], -1)
    near_w = extend(projected)
    basis = jnp.concatenate([modes_x, projected, previous_p], axis=0)
    stiff_basis = jnp.concatenate([stiff_x, apply_blocks(stiff, near_w), stiff_p], axis=0)
    mass_basis = jnp.concatenate([mass_x, apply_blocks(mass, near_w), mass_p], axis=0)
    part_k = jnp.dot(basis.astype(jnp.float32), stiff_basis.T.astype(jnp.float32), precision=HIGH, preferred_element_type=jnp.float32)
    part_m = jnp.dot(basis.astype(jnp.float32), mass_basis.T.astype(jnp.float32), precision=HIGH, preferred_element_type=jnp.float32)
    gram_k = 0.5 * (part_k + part_k.T)
    gram_m = 0.5 * (part_m + part_m.T)
    factor = jnp.linalg.cholesky(gram_m)
    left = jax.scipy.linalg.solve_triangular(factor, gram_k, lower=True)
    reduced = jax.scipy.linalg.solve_triangular(factor, left.T, lower=True)
    return (projected, reduced)
```

```python
import jax
import jax.numpy as jnp
from jax import lax
from jax.sharding import PartitionSpec as P

BLOCK = 128
SWEEPS = 4
NODE_DEV = 1024
SLOTS = 256
TABLE = 1536


HIGH = lax.Precision.HIGHEST
OMEGA = 0.6


def from_behind(value, axis, steps):
    count = lax.axis_size(axis)
    initial, last = (max(0, -steps), min(count, count - steps))
    return lax.ppermute(value, axis, [(source, source + steps) for source in range(initial, last)])


def all_sum(value):
    for axis in ("gx", "gy"):
        count = lax.axis_size(axis)
        if count & (count - 1):
            value = lax.psum(value, axis)
            continue
        step = 1
        while step < count:
            value = value + lax.ppermute(value, axis, [(i, i ^ step) for i in range(count)])
            step *= 2
    return value


def extend_field(field):
    length = field.shape[1]
    pieces = [field]
    for offset in (1, -1):
        face = field[:, length - BLOCK :] if offset == 1 else field[:, :BLOCK]
        pieces.append(from_behind(face, "gx", offset))
    for offset in (1, -1):
        face = (
            field[:, length - 2 * BLOCK : length - BLOCK]
            if offset == 1
            else field[:, BLOCK : 2 * BLOCK]
        )
        pieces.append(from_behind(face, "gy", offset))
    return jnp.concatenate(pieces, axis=1)


def apply_blocks(blocks, pattern, extended):
    vectors = extended.shape[0]
    tiles = extended.reshape(vectors, -1, BLOCK)
    picked = tiles[:, pattern]
    result = jnp.einsum("vrkj,rkij->vri", picked, blocks, precision=HIGH)
    return result.reshape(vectors, -1)


def split3(x):
    hi = lax.reduce_precision(x, exponent_bits=8, mantissa_bits=7)
    rest = x - hi
    mid = lax.reduce_precision(rest, exponent_bits=8, mantissa_bits=7)
    lo = rest - mid
    return jnp.concatenate([hi, mid, lo], axis=0).astype(jnp.bfloat16)


def exact_dot(x, matrix, contract):
    rows = x.shape[0]
    out = lax.dot_general(
        split3(x), matrix, (((1,), (contract,)), ((), ())), preferred_element_type=jnp.float32
    )
    return (out[:rows] + out[rows : 2 * rows]) + out[2 * rows :]


def toward_owners(buffer):
    sections = []
    for direction in range(4):
        section = buffer[:, direction * SLOTS : (direction + 1) * SLOTS]
        if direction < 2:
            sections.append(from_behind(section, "gx", 2 * direction - 1))
        else:
            sections.append(from_behind(section, "gy", 2 * direction - 5))
    return jnp.concatenate(sections, axis=1)


def toward_ghosts(buffer):
    sections = []
    for direction in range(4):
        section = buffer[:, direction * SLOTS : (direction + 1) * SLOTS]
        if direction < 2:
            sections.append(from_behind(section, "gx", 1 - 2 * direction))
        else:
            sections.append(from_behind(section, "gy", 5 - 2 * direction))
    return jnp.concatenate(sections, axis=1)


def body(
    modes_x,
    previous_p,
    stiff_blocks,
    mass_blocks,
    block_pattern,
    lumped_mass,
    edge_ends,
    ghost_slot,
    owner_node,
):
    vectors = modes_x.shape[0]
    ghosts = ghost_slot.shape[0]
    slots = owner_node.shape[0]
    width = NODE_DEV + slots

    def column(index):
        ghost = jnp.clip(index - NODE_DEV, 0, ghosts - 1)
        return jnp.where(index < NODE_DEV, index, NODE_DEV + ghost_slot[ghost])

    columns = lax.broadcasted_iota(jnp.int32, (1, width), 1)
    heads = column(edge_ends[1])[:, None] == columns
    tails = column(edge_ends[0])[:, None] == columns
    grad_matrix = heads.astype(jnp.bfloat16) - tails.astype(jnp.bfloat16)
    touch_matrix = (heads | tails).astype(jnp.bfloat16)
    nodes = lax.broadcasted_iota(jnp.int32, (NODE_DEV, 1), 0)
    owner_matrix = (nodes == owner_node[None, :]).astype(jnp.bfloat16)

    def gradient(owned):
        received = toward_ghosts(exact_dot(owned, owner_matrix, 0))
        table = jnp.concatenate([owned, received], axis=1)
        return exact_dot(table, grad_matrix, 1)

    def gather_owned(local):
        received = toward_owners(local[:, NODE_DEV:])
        return local[:, :NODE_DEV] + exact_dot(received, owner_matrix, 1)

    both = jnp.concatenate([modes_x, previous_p], axis=0)
    near = extend_field(both)
    stiff_both = apply_blocks(stiff_blocks, block_pattern, near)
    mass_both = apply_blocks(mass_blocks, block_pattern, near)
    stiff_x, stiff_p = stiff_both[:vectors], stiff_both[vectors:]
    mass_x, mass_p = mass_both[:vectors], mass_both[vectors:]
    upper, lower = jnp.split(
        all_sum(jnp.concatenate([jnp.sum(modes_x * stiff_x, axis=1), jnp.sum(modes_x * mass_x, axis=1)])), 2
    )
    ritz = upper / lower
    residual = stiff_x - ritz[:, None] * mass_x
    mass_r = apply_blocks(mass_blocks, block_pattern, extend_field(residual))

    rhs_local = exact_dot(mass_r, grad_matrix, 0)
    weight_local = exact_dot(lumped_mass[None], touch_matrix, 0)
    owned_both = gather_owned(jnp.concatenate([rhs_local, weight_local], axis=0))
    rhs = owned_both[:vectors]
    diagonal = owned_both[vectors:]
    potential = OMEGA * rhs / diagonal
    for sweep in range(SWEEPS - 1):
        flux = lumped_mass[None] * gradient(potential)
        applied = gather_owned(exact_dot(flux, grad_matrix, 0))
        potential = potential + OMEGA * (rhs - applied) / diagonal
    projected = residual - gradient(potential)

    near_w = extend_field(projected)
    stiff_w = apply_blocks(stiff_blocks, block_pattern, near_w)
    mass_w = apply_blocks(mass_blocks, block_pattern, near_w)
    basis = jnp.concatenate([modes_x, projected, previous_p], axis=0)
    stiff_basis = jnp.concatenate([stiff_x, stiff_w, stiff_p], axis=0)
    mass_basis = jnp.concatenate([mass_x, mass_w, mass_p], axis=0)
    part_k = jnp.dot(basis, stiff_basis.T, precision=HIGH, preferred_element_type=jnp.float32)
    part_m = jnp.dot(basis, mass_basis.T, precision=HIGH, preferred_element_type=jnp.float32)
    summed_k, summed_m = all_sum(jnp.stack([part_k, part_m]))
    gram_k = 0.5 * (summed_k + summed_k.T)
    gram_m = 0.5 * (summed_m + summed_m.T)
    factor = jnp.linalg.cholesky(gram_m)
    left = jax.scipy.linalg.solve_triangular(factor, gram_k, lower=True)
    reduced = jax.scipy.linalg.solve_triangular(factor, left.T, lower=True)
    return (projected, reduced)


def solution(mesh):
    placed = (
        P(None, ("gx", "gy")),
        P(None, ("gx", "gy")),
        P(("gx", "gy"), None, None, None),
        P(("gx", "gy"), None, None, None),
        P(("gx", "gy"), None),
        P(("gx", "gy")),
        P(None, ("gx", "gy")),
        P(("gx", "gy")),
        P(("gx", "gy")),
    )
    return jax.shard_map(
        body, mesh=mesh, in_specs=placed, out_specs=(P(None, ("gx", "gy")), P()), check_vma=False
    )
```

```python
import jax
import jax.numpy as jnp
from jax import lax
from jax.sharding import PartitionSpec as P

BLOCK = 128
SWEEPS = 4
NODE_DEV = 1024
SLOTS = 256
TABLE = 1536


HIGH = lax.Precision.HIGHEST
OMEGA = 0.6


def from_behind(value, axis, steps):
    count = lax.axis_size(axis)
    initial, last = (max(0, -steps), min(count, count - steps))
    return lax.ppermute(value, axis, [(source, source + steps) for source in range(initial, last)])


def all_sum(value):
    for axis in ("gx", "gy"):
        count = lax.axis_size(axis)
        if count & (count - 1):
            value = lax.psum(value, axis)
            continue
        step = 1
        while step < count:
            value = value + lax.ppermute(value, axis, [(i, i ^ step) for i in range(count)])
            step *= 2
    return value


def extend_field(field):
    length = field.shape[1]
    pieces = [field]
    for offset in (1, -1):
        face = field[:, length - BLOCK :] if offset == 1 else field[:, :BLOCK]
        pieces.append(from_behind(face, "gx", offset))
    for offset in (1, -1):
        face = (
            field[:, length - 2 * BLOCK : length - BLOCK]
            if offset == 1
            else field[:, BLOCK : 2 * BLOCK]
        )
        pieces.append(from_behind(face, "gy", offset))
    return jnp.concatenate(pieces, axis=1)


def apply_blocks(blocks, pattern, extended):
    vectors = extended.shape[0]
    tiles = extended.reshape(vectors, -1, BLOCK)
    picked = tiles[:, pattern]
    result = jnp.einsum("vrkj,rkij->vri", picked, blocks, precision=HIGH)
    return result.reshape(vectors, -1)


def split3(x):
    hi = lax.reduce_precision(x, exponent_bits=8, mantissa_bits=7)
    rest = x - hi
    mid = lax.reduce_precision(rest, exponent_bits=8, mantissa_bits=7)
    lo = rest - mid
    return jnp.concatenate([hi, mid, lo], axis=0).astype(jnp.bfloat16)


def exact_dot(x, matrix, contract):
    rows = x.shape[0]
    out = lax.dot_general(
        split3(x), matrix.astype(jnp.bfloat16), (((1,), (contract,)), ((), ())), preferred_element_type=jnp.float32
    )
    return (out[:rows] + out[rows : 2 * rows]) + out[2 * rows :]


def toward_owners(buffer):
    sections = []
    for direction in range(4):
        section = buffer[:, direction * SLOTS : (direction + 1) * SLOTS]
        if direction < 2:
            sections.append(from_behind(section, "gx", 2 * direction - 1))
        else:
            sections.append(from_behind(section, "gy", 2 * direction - 5))
    return jnp.concatenate(sections, axis=1)


def toward_ghosts(buffer):
    sections = []
    for direction in range(4):
        section = buffer[:, direction * SLOTS : (direction + 1) * SLOTS]
        if direction < 2:
            sections.append(from_behind(section, "gx", 1 - 2 * direction))
        else:
            sections.append(from_behind(section, "gy", 5 - 2 * direction))
    return jnp.concatenate(sections, axis=1)


def body(
    modes_x,
    previous_p,
    stiff_blocks,
    mass_blocks,
    block_pattern,
    lumped_mass,
    edge_ends,
    ghost_slot,
    owner_node,
):
    vectors = modes_x.shape[0]
    ghosts = ghost_slot.shape[0]
    slots = owner_node.shape[0]
    width = NODE_DEV + slots

    def column(index):
        ghost = index - NODE_DEV
        pick = (ghost[:, None] == lax.broadcasted_iota(jnp.int32, (1, ghosts), 1)).astype(jnp.bfloat16)
        parts = jnp.stack([ghost_slot // 32, ghost_slot % 32], axis=1).astype(jnp.bfloat16)
        got = jnp.dot(pick, parts, preferred_element_type=jnp.float32)
        slot = (got[:, 0] * 32 + got[:, 1]).astype(jnp.int32)
        return jnp.where(index < NODE_DEV, index, NODE_DEV + slot)

    ends = column(edge_ends.reshape(-1)).reshape(2, -1)
    columns = lax.broadcasted_iota(jnp.int32, (1, width), 1)
    heads = ends[1][:, None] == columns
    tails = ends[0][:, None] == columns
    grad_matrix, touch_matrix = lax.optimization_barrier(
        (heads.astype(jnp.int8) - tails.astype(jnp.int8), (heads | tails).astype(jnp.int8))
    )
    nodes = lax.broadcasted_iota(jnp.int32, (NODE_DEV, 1), 0)
    owner_matrix = (nodes == owner_node[None, :]).astype(jnp.bfloat16)

    def gradient(owned):
        received = toward_ghosts(exact_dot(owned, owner_matrix, 0))
        table = jnp.concatenate([owned, received], axis=1)
        return exact_dot(table, grad_matrix, 1)

    def gather_owned(local):
        received = toward_owners(local[:, NODE_DEV:])
        return local[:, :NODE_DEV] + exact_dot(received, owner_matrix, 1)

    both = jnp.concatenate([modes_x, previous_p], axis=0)
    near = extend_field(both)
    stiff_both = apply_blocks(stiff_blocks, block_pattern, near)
    mass_both = apply_blocks(mass_blocks, block_pattern, near)
    stiff_x, stiff_p = stiff_both[:vectors], stiff_both[vectors:]
    mass_x, mass_p = mass_both[:vectors], mass_both[vectors:]
    upper, lower = jnp.split(
        all_sum(jnp.concatenate([jnp.sum(modes_x * stiff_x, axis=1), jnp.sum(modes_x * mass_x, axis=1)])), 2
    )
    ritz = upper / lower
    residual = stiff_x - ritz[:, None] * mass_x
    mass_r = apply_blocks(mass_blocks, block_pattern, extend_field(residual))

    rhs_local = exact_dot(mass_r, grad_matrix, 0)
    weight_local = exact_dot(lumped_mass[None], touch_matrix, 0)
    owned_both = gather_owned(jnp.concatenate([rhs_local, weight_local], axis=0))
    rhs = owned_both[:vectors]
    diagonal = owned_both[vectors:]
    potential = OMEGA * rhs / diagonal
    for sweep in range(SWEEPS - 1):
        flux = lumped_mass[None] * gradient(potential)
        applied = gather_owned(exact_dot(flux, grad_matrix, 0))
        potential = potential + OMEGA * (rhs - applied) / diagonal
    projected = residual - gradient(potential)

    near_w = extend_field(projected)
    stiff_w = apply_blocks(stiff_blocks, block_pattern, near_w)
    mass_w = apply_blocks(mass_blocks, block_pattern, near_w)
    basis = jnp.concatenate([modes_x, projected, previous_p], axis=0)
    stiff_basis = jnp.concatenate([stiff_x, stiff_w, stiff_p], axis=0)
    mass_basis = jnp.concatenate([mass_x, mass_w, mass_p], axis=0)
    part_k = jnp.dot(basis, stiff_basis.T, precision=HIGH, preferred_element_type=jnp.float32)
    part_m = jnp.dot(basis, mass_basis.T, precision=HIGH, preferred_element_type=jnp.float32)
    summed_k, summed_m = all_sum(jnp.stack([part_k, part_m]))
    gram_k = 0.5 * (summed_k + summed_k.T)
    gram_m = 0.5 * (summed_m + summed_m.T)
    factor = jnp.linalg.cholesky(gram_m)
    left = jax.scipy.linalg.solve_triangular(factor, gram_k, lower=True)
    reduced = jax.scipy.linalg.solve_triangular(factor, left.T, lower=True)
    return (projected, reduced)


def solution(mesh):
    placed = (
        P(None, ("gx", "gy")),
        P(None, ("gx", "gy")),
        P(("gx", "gy"), None, None, None),
        P(("gx", "gy"), None, None, None),
        P(("gx", "gy"), None),
        P(("gx", "gy")),
        P(None, ("gx", "gy")),
        P(("gx", "gy")),
        P(("gx", "gy")),
    )
    return jax.shard_map(
        body, mesh=mesh, in_specs=placed, out_specs=(P(None, ("gx", "gy")), P()), check_vma=False
    )
```

```python
import jax
import jax.numpy as jnp
from jax import lax
from jax.sharding import PartitionSpec as P

BLOCK = 128
SWEEPS = 4
NODE_DEV = 1024
SLOTS = 256
TABLE = 1536


HIGH = lax.Precision.HIGHEST
OMEGA = 0.6


def from_behind(value, axis, steps):
    count = lax.axis_size(axis)
    received = lax.ppermute(value, axis, [(source, (source + steps) % count) for source in range(count)])
    place = lax.axis_index(axis) - steps
    return jnp.where((place >= 0) & (place < count), received, 0.0)


def all_sum(value):
    for axis in ("gx", "gy"):
        count = lax.axis_size(axis)
        if count & (count - 1):
            value = lax.psum(value, axis)
            continue
        step = 1
        while step < count:
            value = value + lax.ppermute(value, axis, [(i, i ^ step) for i in range(count)])
            step *= 2
    return value


def extend_field(field):
    length = field.shape[1]
    pieces = [field]
    for offset in (1, -1):
        face = field[:, length - BLOCK :] if offset == 1 else field[:, :BLOCK]
        pieces.append(from_behind(face, "gx", offset))
    for offset in (1, -1):
        face = (
            field[:, length - 2 * BLOCK : length - BLOCK]
            if offset == 1
            else field[:, BLOCK : 2 * BLOCK]
        )
        pieces.append(from_behind(face, "gy", offset))
    return jnp.concatenate(pieces, axis=1)


def apply_blocks(blocks, pattern, extended):
    vectors = extended.shape[0]
    tiles = extended.reshape(vectors, -1, BLOCK)
    picked = tiles[:, pattern]
    result = jnp.einsum("vrkj,rkij->vri", picked, blocks, precision=HIGH)
    return result.reshape(vectors, -1)


def split3(x):
    hi = lax.reduce_precision(x, exponent_bits=8, mantissa_bits=7)
    rest = x - hi
    mid = lax.reduce_precision(rest, exponent_bits=8, mantissa_bits=7)
    lo = rest - mid
    return jnp.concatenate([hi, mid, lo], axis=0).astype(jnp.bfloat16)


def exact_dot(x, matrix, contract):
    rows = x.shape[0]
    out = lax.dot_general(
        split3(x), matrix.astype(jnp.bfloat16), (((1,), (contract,)), ((), ())), preferred_element_type=jnp.float32
    )
    return (out[:rows] + out[rows : 2 * rows]) + out[2 * rows :]


def toward_owners(buffer):
    sections = []
    for direction in range(4):
        section = buffer[:, direction * SLOTS : (direction + 1) * SLOTS]
        if direction < 2:
            sections.append(from_behind(section, "gx", 2 * direction - 1))
        else:
            sections.append(from_behind(section, "gy", 2 * direction - 5))
    return jnp.concatenate(sections, axis=1)


def toward_ghosts(buffer):
    sections = []
    for direction in range(4):
        section = buffer[:, direction * SLOTS : (direction + 1) * SLOTS]
        if direction < 2:
            sections.append(from_behind(section, "gx", 1 - 2 * direction))
        else:
            sections.append(from_behind(section, "gy", 5 - 2 * direction))
    return jnp.concatenate(sections, axis=1)


def body(
    modes_x,
    previous_p,
    stiff_blocks,
    mass_blocks,
    block_pattern,
    lumped_mass,
    edge_ends,
    ghost_slot,
    owner_node,
):
    vectors = modes_x.shape[0]
    ghosts = ghost_slot.shape[0]
    slots = owner_node.shape[0]
    width = NODE_DEV + slots

    def column(index):
        ghost = index - NODE_DEV
        pick = (ghost[:, None] == lax.broadcasted_iota(jnp.int32, (1, ghosts), 1)).astype(jnp.bfloat16)
        parts = jnp.stack([ghost_slot // 32, ghost_slot % 32], axis=1).astype(jnp.bfloat16)
        got = jnp.dot(pick, parts, preferred_element_type=jnp.float32)
        slot = (got[:, 0] * 32 + got[:, 1]).astype(jnp.int32)
        return jnp.where(index < NODE_DEV, index, NODE_DEV + slot)

    ends = column(edge_ends.reshape(-1)).reshape(2, -1)
    columns = lax.broadcasted_iota(jnp.int32, (1, width), 1)
    heads = ends[1][:, None] == columns
    tails = ends[0][:, None] == columns
    grad_matrix = lax.optimization_barrier(heads.astype(jnp.int8) - tails.astype(jnp.int8))
    nodes = lax.broadcasted_iota(jnp.int32, (NODE_DEV, 1), 0)
    owner_matrix = (nodes == owner_node[None, :]).astype(jnp.bfloat16)

    def gradient(owned):
        received = toward_ghosts(exact_dot(owned, owner_matrix, 0))
        table = jnp.concatenate([owned, received], axis=1)
        return exact_dot(table, grad_matrix, 1)

    def gather_owned(local):
        received = toward_owners(local[:, NODE_DEV:])
        return local[:, :NODE_DEV] + exact_dot(received, owner_matrix, 1)

    both = jnp.concatenate([modes_x, previous_p], axis=0)
    near = extend_field(both)
    stiff_both = apply_blocks(stiff_blocks, block_pattern, near)
    mass_both = apply_blocks(mass_blocks, block_pattern, near)
    stiff_x, stiff_p = stiff_both[:vectors], stiff_both[vectors:]
    mass_x, mass_p = mass_both[:vectors], mass_both[vectors:]
    upper, lower = jnp.split(
        all_sum(jnp.concatenate([jnp.sum(modes_x * stiff_x, axis=1), jnp.sum(modes_x * mass_x, axis=1)])), 2
    )
    ritz = upper / lower
    residual = stiff_x - ritz[:, None] * mass_x
    mass_r = apply_blocks(mass_blocks, block_pattern, extend_field(residual))

    rhs_local = exact_dot(mass_r, grad_matrix, 0)
    weight_local = exact_dot(lumped_mass[None], jnp.abs(grad_matrix), 0)
    owned_both = gather_owned(jnp.concatenate([rhs_local, weight_local], axis=0))
    rhs = owned_both[:vectors]
    diagonal = owned_both[vectors:]
    potential = OMEGA * rhs / diagonal
    for sweep in range(SWEEPS - 1):
        flux = lumped_mass[None] * gradient(potential)
        applied = gather_owned(exact_dot(flux, grad_matrix, 0))
        potential = potential + OMEGA * (rhs - applied) / diagonal
    projected = residual - gradient(potential)

    near_w = extend_field(projected)
    stiff_w = apply_blocks(stiff_blocks, block_pattern, near_w)
    mass_w = apply_blocks(mass_blocks, block_pattern, near_w)
    basis = jnp.concatenate([modes_x, projected, previous_p], axis=0)
    stiff_basis = jnp.concatenate([stiff_x, stiff_w, stiff_p], axis=0)
    mass_basis = jnp.concatenate([mass_x, mass_w, mass_p], axis=0)
    part_k = jnp.dot(basis, stiff_basis.T, precision=HIGH, preferred_element_type=jnp.float32)
    part_m = jnp.dot(basis, mass_basis.T, precision=HIGH, preferred_element_type=jnp.float32)
    summed_k, summed_m = all_sum(jnp.stack([part_k, part_m]))
    gram_k = 0.5 * (summed_k + summed_k.T)
    gram_m = 0.5 * (summed_m + summed_m.T)
    factor = jnp.linalg.cholesky(gram_m)
    left = jax.scipy.linalg.solve_triangular(factor, gram_k, lower=True)
    reduced = jax.scipy.linalg.solve_triangular(factor, left.T, lower=True)
    return (projected, reduced)


def solution(mesh):
    placed = (
        P(None, ("gx", "gy")),
        P(None, ("gx", "gy")),
        P(("gx", "gy"), None, None, None),
        P(("gx", "gy"), None, None, None),
        P(("gx", "gy"), None),
        P(("gx", "gy")),
        P(None, ("gx", "gy")),
        P(("gx", "gy")),
        P(("gx", "gy")),
    )
    return jax.shard_map(
        body, mesh=mesh, in_specs=placed, out_specs=(P(None, ("gx", "gy")), P()), check_vma=False
    )
```

```python
import jax
import jax.numpy as jnp
from jax import lax
from jax.sharding import PartitionSpec as P
from jax.experimental import pallas as pl
from jax.experimental.pallas import tpu as pltpu

BLOCK = 128
SWEEPS = 4
NODE_DEV = 1024
SLOTS = 256
TABLE = 1536


HIGH = lax.Precision.HIGHEST
OMEGA = 0.6


def from_behind(value, axis, steps):
    count = lax.axis_size(axis)
    received = lax.ppermute(value, axis, [(source, (source + steps) % count) for source in range(count)])
    place = lax.axis_index(axis) - steps
    return jnp.where((place >= 0) & (place < count), received, 0.0)


def all_sum(value):
    for axis in ("gx", "gy"):
        count = lax.axis_size(axis)
        if count & (count - 1):
            value = lax.psum(value, axis)
            continue
        step = 1
        while step < count:
            value = value + lax.ppermute(value, axis, [(i, i ^ step) for i in range(count)])
            step *= 2
    return value


def extend_field(field):
    length = field.shape[1]
    pieces = [field]
    for offset in (1, -1):
        face = field[:, length - BLOCK :] if offset == 1 else field[:, :BLOCK]
        pieces.append(from_behind(face, "gx", offset))
    for offset in (1, -1):
        face = (
            field[:, length - 2 * BLOCK : length - BLOCK]
            if offset == 1
            else field[:, BLOCK : 2 * BLOCK]
        )
        pieces.append(from_behind(face, "gy", offset))
    return jnp.concatenate(pieces, axis=1)


def block_kernel(pattern_ref, extended_ref, *refs):
    count = len(refs) // 2
    matrices, outputs = refs[:count], refs[count:]
    rows, per_row = matrices[0].shape[0], matrices[0].shape[1]
    step = pl.program_id(0)
    for row in range(rows):
        base = (step * rows + row) * per_row
        picked = [extended_ref[pattern_ref[base + k]] for k in range(per_row)]
        for matrix, output in zip(matrices, outputs):
            total = None
            for k in range(per_row):
                term = lax.dot_general(
                    picked[k], matrix[row, k], (((1,), (1,)), ((), ())),
                    precision=HIGH, preferred_element_type=jnp.float32,
                )
                total = term if total is None else total + term
            output[:, row * BLOCK : (row + 1) * BLOCK] = total


def apply_blocks(block_sets, pattern, extended, rows_per_step=4):
    vectors = extended.shape[0]
    columns = extended.shape[1] // BLOCK
    row_blocks, per_row = block_sets[0].shape[0], block_sets[0].shape[1]
    stacked = extended.reshape(vectors, columns, BLOCK).transpose(1, 0, 2)
    grid = pltpu.PrefetchScalarGridSpec(
        num_scalar_prefetch=1,
        grid=(row_blocks // rows_per_step,),
        in_specs=[pl.BlockSpec((columns, vectors, BLOCK), lambda i, p: (0, 0, 0))]
        + [pl.BlockSpec((rows_per_step, per_row, BLOCK, BLOCK), lambda i, p: (i, 0, 0, 0)) for _ in block_sets],
        out_specs=[pl.BlockSpec((vectors, rows_per_step * BLOCK), lambda i, p: (0, i)) for _ in block_sets],
    )
    return pl.pallas_call(
        block_kernel,
        grid_spec=grid,
        out_shape=[jax.ShapeDtypeStruct((vectors, row_blocks * BLOCK), jnp.float32) for _ in block_sets],
    )(pattern.reshape(-1), stacked, *block_sets)


def split3(x):
    hi = lax.reduce_precision(x, exponent_bits=8, mantissa_bits=7)
    rest = x - hi
    mid = lax.reduce_precision(rest, exponent_bits=8, mantissa_bits=7)
    lo = rest - mid
    return jnp.concatenate([hi, mid, lo], axis=0).astype(jnp.bfloat16)


def exact_dot(x, matrix, contract):
    rows = x.shape[0]
    out = lax.dot_general(
        split3(x), matrix.astype(jnp.bfloat16), (((1,), (contract,)), ((), ())), preferred_element_type=jnp.float32
    )
    return (out[:rows] + out[rows : 2 * rows]) + out[2 * rows :]


def toward_owners(buffer):
    sections = []
    for direction in range(4):
        section = buffer[:, direction * SLOTS : (direction + 1) * SLOTS]
        if direction < 2:
            sections.append(from_behind(section, "gx", 2 * direction - 1))
        else:
            sections.append(from_behind(section, "gy", 2 * direction - 5))
    return jnp.concatenate(sections, axis=1)


def toward_ghosts(buffer):
    sections = []
    for direction in range(4):
        section = buffer[:, direction * SLOTS : (direction + 1) * SLOTS]
        if direction < 2:
            sections.append(from_behind(section, "gx", 1 - 2 * direction))
        else:
            sections.append(from_behind(section, "gy", 5 - 2 * direction))
    return jnp.concatenate(sections, axis=1)


def body(
    modes_x,
    previous_p,
    stiff_blocks,
    mass_blocks,
    block_pattern,
    lumped_mass,
    edge_ends,
    ghost_slot,
    owner_node,
):
    vectors = modes_x.shape[0]
    ghosts = ghost_slot.shape[0]
    slots = owner_node.shape[0]
    width = NODE_DEV + slots

    def column(index):
        ghost = index - NODE_DEV
        pick = (ghost[:, None] == lax.broadcasted_iota(jnp.int32, (1, ghosts), 1)).astype(jnp.bfloat16)
        parts = jnp.stack([ghost_slot // 32, ghost_slot % 32], axis=1).astype(jnp.bfloat16)
        got = jnp.dot(pick, parts, preferred_element_type=jnp.float32)
        slot = (got[:, 0] * 32 + got[:, 1]).astype(jnp.int32)
        return jnp.where(index < NODE_DEV, index, NODE_DEV + slot)

    ends = column(edge_ends.reshape(-1)).reshape(2, -1)
    columns = lax.broadcasted_iota(jnp.int32, (1, width), 1)
    heads = ends[1][:, None] == columns
    tails = ends[0][:, None] == columns
    grad_matrix = lax.optimization_barrier(heads.astype(jnp.int8) - tails.astype(jnp.int8))
    nodes = lax.broadcasted_iota(jnp.int32, (NODE_DEV, 1), 0)
    owner_matrix = (nodes == owner_node[None, :]).astype(jnp.bfloat16)

    def gradient(owned):
        received = toward_ghosts(exact_dot(owned, owner_matrix, 0))
        table = jnp.concatenate([owned, received], axis=1)
        return exact_dot(table, grad_matrix, 1)

    def gather_owned(local):
        received = toward_owners(local[:, NODE_DEV:])
        return local[:, :NODE_DEV] + exact_dot(received, owner_matrix, 1)

    both = jnp.concatenate([modes_x, previous_p], axis=0)
    near = extend_field(both)
    stiff_both, mass_both = apply_blocks((stiff_blocks, mass_blocks), block_pattern, near)
    stiff_x, stiff_p = stiff_both[:vectors], stiff_both[vectors:]
    mass_x, mass_p = mass_both[:vectors], mass_both[vectors:]
    upper, lower = jnp.split(
        all_sum(jnp.concatenate([jnp.sum(modes_x * stiff_x, axis=1), jnp.sum(modes_x * mass_x, axis=1)])), 2
    )
    ritz = upper / lower
    residual = stiff_x - ritz[:, None] * mass_x
    (mass_r,) = apply_blocks((mass_blocks,), block_pattern, extend_field(residual))

    rhs_local = exact_dot(mass_r, grad_matrix, 0)
    weight_local = exact_dot(lumped_mass[None], jnp.abs(grad_matrix), 0)
    owned_both = gather_owned(jnp.concatenate([rhs_local, weight_local], axis=0))
    rhs = owned_both[:vectors]
    diagonal = owned_both[vectors:]
    potential = OMEGA * rhs / diagonal
    for sweep in range(SWEEPS - 1):
        flux = lumped_mass[None] * gradient(potential)
        applied = gather_owned(exact_dot(flux, grad_matrix, 0))
        potential = potential + OMEGA * (rhs - applied) / diagonal
    projected = residual - gradient(potential)

    near_w = extend_field(projected)
    stiff_w, mass_w = apply_blocks((stiff_blocks, mass_blocks), block_pattern, near_w)
    basis = jnp.concatenate([modes_x, projected, previous_p], axis=0)
    stiff_basis = jnp.concatenate([stiff_x, stiff_w, stiff_p], axis=0)
    mass_basis = jnp.concatenate([mass_x, mass_w, mass_p], axis=0)
    part_k = jnp.dot(basis, stiff_basis.T, precision=HIGH, preferred_element_type=jnp.float32)
    part_m = jnp.dot(basis, mass_basis.T, precision=HIGH, preferred_element_type=jnp.float32)
    summed_k, summed_m = all_sum(jnp.stack([part_k, part_m]))
    gram_k = 0.5 * (summed_k + summed_k.T)
    gram_m = 0.5 * (summed_m + summed_m.T)
    factor = jnp.linalg.cholesky(gram_m)
    left = jax.scipy.linalg.solve_triangular(factor, gram_k, lower=True)
    reduced = jax.scipy.linalg.solve_triangular(factor, left.T, lower=True)
    return (projected, reduced)


def solution(mesh):
    placed = (
        P(None, ("gx", "gy")),
        P(None, ("gx", "gy")),
        P(("gx", "gy"), None, None, None),
        P(("gx", "gy"), None, None, None),
        P(("gx", "gy"), None),
        P(("gx", "gy")),
        P(None, ("gx", "gy")),
        P(("gx", "gy")),
        P(("gx", "gy")),
    )
    return jax.shard_map(
        body, mesh=mesh, in_specs=placed, out_specs=(P(None, ("gx", "gy")), P()), check_vma=False
    )
```

```python
import jax
import jax.numpy as jnp
from jax import lax
from jax.sharding import PartitionSpec as P

BLOCK = 128
SWEEPS = 4
NODE_DEV = 1024
SLOTS = 256
TABLE = 1536


HIGH = lax.Precision.HIGHEST
OMEGA = 0.6


def from_behind(value, axis, steps):
    count = lax.axis_size(axis)
    received = lax.ppermute(value, axis, [(source, (source + steps) % count) for source in range(count)])
    place = lax.axis_index(axis) - steps
    return jnp.where((place >= 0) & (place < count), received, 0.0)


def all_sum(value):
    for axis in ("gx", "gy"):
        count = lax.axis_size(axis)
        if count & (count - 1):
            value = lax.psum(value, axis)
            continue
        step = 1
        while step < count:
            value = value + lax.ppermute(value, axis, [(i, i ^ step) for i in range(count)])
            step *= 2
    return value


def exchange_faces(field):
    length = field.shape[1]
    pieces = []
    for offset in (1, -1):
        face = field[:, length - BLOCK :] if offset == 1 else field[:, :BLOCK]
        pieces.append(from_behind(face, "gx", offset))
    for offset in (1, -1):
        face = (
            field[:, length - 2 * BLOCK : length - BLOCK]
            if offset == 1
            else field[:, BLOCK : 2 * BLOCK]
        )
        pieces.append(from_behind(face, "gy", offset))
    return jnp.concatenate(pieces, axis=1)


def extend_field(field):
    return jnp.concatenate([field, exchange_faces(field)], axis=1)


def apply_blocks(blocks, pattern, extended):
    vectors = extended.shape[0]
    tiles = extended.reshape(vectors, -1, BLOCK)
    picked = tiles[:, pattern]
    result = jnp.einsum("vrkj,rkij->vri", picked, blocks, precision=HIGH)
    return result.reshape(vectors, -1)


def split3(x):
    hi = lax.reduce_precision(x, exponent_bits=8, mantissa_bits=7)
    rest = x - hi
    mid = lax.reduce_precision(rest, exponent_bits=8, mantissa_bits=7)
    lo = rest - mid
    return jnp.concatenate([hi, mid, lo], axis=0).astype(jnp.bfloat16)


def exact_dot(x, matrix, contract):
    rows = x.shape[0]
    out = lax.dot_general(
        split3(x), matrix.astype(jnp.bfloat16), (((1,), (contract,)), ((), ())), preferred_element_type=jnp.float32
    )
    return (out[:rows] + out[rows : 2 * rows]) + out[2 * rows :]


def toward_owners(buffer):
    sections = []
    for direction in range(4):
        section = buffer[:, direction * SLOTS : (direction + 1) * SLOTS]
        if direction < 2:
            sections.append(from_behind(section, "gx", 2 * direction - 1))
        else:
            sections.append(from_behind(section, "gy", 2 * direction - 5))
    return jnp.concatenate(sections, axis=1)


def toward_ghosts(buffer):
    sections = []
    for direction in range(4):
        section = buffer[:, direction * SLOTS : (direction + 1) * SLOTS]
        if direction < 2:
            sections.append(from_behind(section, "gx", 1 - 2 * direction))
        else:
            sections.append(from_behind(section, "gy", 5 - 2 * direction))
    return jnp.concatenate(sections, axis=1)


def body(
    modes_x,
    previous_p,
    stiff_blocks,
    mass_blocks,
    block_pattern,
    lumped_mass,
    edge_ends,
    ghost_slot,
    owner_node,
):
    vectors = modes_x.shape[0]
    ghosts = ghost_slot.shape[0]
    slots = owner_node.shape[0]
    width = NODE_DEV + slots

    def column(index):
        ghost = index - NODE_DEV
        pick = (ghost[:, None] == lax.broadcasted_iota(jnp.int32, (1, ghosts), 1)).astype(jnp.bfloat16)
        parts = jnp.stack([ghost_slot // 32, ghost_slot % 32], axis=1).astype(jnp.bfloat16)
        got = jnp.dot(pick, parts, preferred_element_type=jnp.float32)
        slot = (got[:, 0] * 32 + got[:, 1]).astype(jnp.int32)
        return jnp.where(index < NODE_DEV, index, NODE_DEV + slot)

    ends = column(edge_ends.reshape(-1)).reshape(2, -1)
    columns = lax.broadcasted_iota(jnp.int32, (1, width), 1)
    heads = ends[1][:, None] == columns
    tails = ends[0][:, None] == columns
    grad_matrix = lax.optimization_barrier(heads.astype(jnp.int8) - tails.astype(jnp.int8))
    nodes = lax.broadcasted_iota(jnp.int32, (NODE_DEV, 1), 0)
    owner_matrix = (nodes == owner_node[None, :]).astype(jnp.bfloat16)

    def gradient(owned):
        received = toward_ghosts(exact_dot(owned, owner_matrix, 0))
        table = jnp.concatenate([owned, received], axis=1)
        return exact_dot(table, grad_matrix, 1)

    def gather_owned(local):
        received = toward_owners(local[:, NODE_DEV:])
        return local[:, :NODE_DEV] + exact_dot(received, owner_matrix, 1)

    both = jnp.concatenate([modes_x, previous_p], axis=0)
    near = extend_field(both)
    stiff_both = apply_blocks(stiff_blocks, block_pattern, near)
    mass_both = apply_blocks(mass_blocks, block_pattern, near)
    stiff_x, stiff_p = stiff_both[:vectors], stiff_both[vectors:]
    mass_x, mass_p = mass_both[:vectors], mass_both[vectors:]
    both_faces = exchange_faces(jnp.concatenate([stiff_x, mass_x], axis=0))
    stiff_faces, mass_faces = both_faces[:vectors], both_faces[vectors:]
    upper, lower = jnp.split(
        all_sum(jnp.concatenate([jnp.sum(modes_x * stiff_x, axis=1), jnp.sum(modes_x * mass_x, axis=1)])), 2
    )
    ritz = upper / lower
    residual = stiff_x - ritz[:, None] * mass_x
    residual_faces = stiff_faces - ritz[:, None] * mass_faces
    mass_r = apply_blocks(mass_blocks, block_pattern, jnp.concatenate([residual, residual_faces], axis=1))

    rhs_local = exact_dot(mass_r, grad_matrix, 0)
    weight_local = exact_dot(lumped_mass[None], jnp.abs(grad_matrix), 0)
    owned_both = gather_owned(jnp.concatenate([rhs_local, weight_local], axis=0))
    rhs = owned_both[:vectors]
    diagonal = owned_both[vectors:]
    potential = OMEGA * rhs / diagonal
    for sweep in range(SWEEPS - 1):
        flux = lumped_mass[None] * gradient(potential)
        applied = gather_owned(exact_dot(flux, grad_matrix, 0))
        potential = potential + OMEGA * (rhs - applied) / diagonal
    projected = residual - gradient(potential)

    near_w = extend_field(projected)
    stiff_w = apply_blocks(stiff_blocks, block_pattern, near_w)
    mass_w = apply_blocks(mass_blocks, block_pattern, near_w)
    basis = jnp.concatenate([modes_x, projected, previous_p], axis=0)
    stiff_basis = jnp.concatenate([stiff_x, stiff_w, stiff_p], axis=0)
    mass_basis = jnp.concatenate([mass_x, mass_w, mass_p], axis=0)
    part_k = jnp.dot(basis, stiff_basis.T, precision=HIGH, preferred_element_type=jnp.float32)
    part_m = jnp.dot(basis, mass_basis.T, precision=HIGH, preferred_element_type=jnp.float32)
    summed_k, summed_m = all_sum(jnp.stack([part_k, part_m]))
    gram_k = 0.5 * (summed_k + summed_k.T)
    gram_m = 0.5 * (summed_m + summed_m.T)
    factor = jnp.linalg.cholesky(gram_m)
    left = jax.scipy.linalg.solve_triangular(factor, gram_k, lower=True)
    reduced = jax.scipy.linalg.solve_triangular(factor, left.T, lower=True)
    return (projected, reduced)


def solution(mesh):
    placed = (
        P(None, ("gx", "gy")),
        P(None, ("gx", "gy")),
        P(("gx", "gy"), None, None, None),
        P(("gx", "gy"), None, None, None),
        P(("gx", "gy"), None),
        P(("gx", "gy")),
        P(None, ("gx", "gy")),
        P(("gx", "gy")),
        P(("gx", "gy")),
    )
    return jax.shard_map(
        body, mesh=mesh, in_specs=placed, out_specs=(P(None, ("gx", "gy")), P()), check_vma=False
    )
```

```python
import jax
import jax.numpy as jnp
from jax import lax
from jax.sharding import PartitionSpec as P

BLOCK = 128
SWEEPS = 4
NODE_DEV = 1024
SLOTS = 256
TABLE = 1536


HIGH = lax.Precision.HIGHEST
OMEGA = 0.6


def from_behind(value, axis, steps):
    count = lax.axis_size(axis)
    received = lax.ppermute(value, axis, [(source, (source + steps) % count) for source in range(count)])
    place = lax.axis_index(axis) - steps
    return jnp.where((place >= 0) & (place < count), received, 0.0)


def all_sum(value):
    for axis in ("gx", "gy"):
        count = lax.axis_size(axis)
        if count & (count - 1):
            value = lax.psum(value, axis)
            continue
        step = 1
        while step < count:
            value = value + lax.ppermute(value, axis, [(i, i ^ step) for i in range(count)])
            step *= 2
    return value


def exchange_faces(field):
    length = field.shape[1]
    pieces = []
    for offset in (1, -1):
        face = field[:, length - BLOCK :] if offset == 1 else field[:, :BLOCK]
        pieces.append(from_behind(face, "gx", offset))
    for offset in (1, -1):
        face = (
            field[:, length - 2 * BLOCK : length - BLOCK]
            if offset == 1
            else field[:, BLOCK : 2 * BLOCK]
        )
        pieces.append(from_behind(face, "gy", offset))
    return jnp.concatenate(pieces, axis=1)


def extend_field(field):
    return jnp.concatenate([field, exchange_faces(field)], axis=1)


def apply_blocks(blocks, pattern, extended):
    vectors = extended.shape[0]
    tiles = extended.reshape(vectors, -1, BLOCK)
    picked = tiles[:, pattern]
    result = jnp.einsum("vrkj,rkij->vri", picked, blocks, precision=lax.Precision.HIGH)
    return result.reshape(vectors, -1)


def split3(x):
    hi = lax.reduce_precision(x, exponent_bits=8, mantissa_bits=7)
    rest = x - hi
    mid = lax.reduce_precision(rest, exponent_bits=8, mantissa_bits=7)
    lo = rest - mid
    return jnp.concatenate([hi, mid, lo], axis=0).astype(jnp.bfloat16)


def exact_dot(x, matrix, contract):
    rows = x.shape[0]
    out = lax.dot_general(
        split3(x), matrix.astype(jnp.bfloat16), (((1,), (contract,)), ((), ())), preferred_element_type=jnp.float32
    )
    return (out[:rows] + out[rows : 2 * rows]) + out[2 * rows :]


def toward_owners(buffer):
    sections = []
    for direction in range(4):
        section = buffer[:, direction * SLOTS : (direction + 1) * SLOTS]
        if direction < 2:
            sections.append(from_behind(section, "gx", 2 * direction - 1))
        else:
            sections.append(from_behind(section, "gy", 2 * direction - 5))
    return jnp.concatenate(sections, axis=1)


def toward_ghosts(buffer):
    sections = []
    for direction in range(4):
        section = buffer[:, direction * SLOTS : (direction + 1) * SLOTS]
        if direction < 2:
            sections.append(from_behind(section, "gx", 1 - 2 * direction))
        else:
            sections.append(from_behind(section, "gy", 5 - 2 * direction))
    return jnp.concatenate(sections, axis=1)


def body(
    modes_x,
    previous_p,
    stiff_blocks,
    mass_blocks,
    block_pattern,
    lumped_mass,
    edge_ends,
    ghost_slot,
    owner_node,
):
    vectors = modes_x.shape[0]
    ghosts = ghost_slot.shape[0]
    slots = owner_node.shape[0]
    width = NODE_DEV + slots

    def column(index):
        ghost = index - NODE_DEV
        pick = (ghost[:, None] == lax.broadcasted_iota(jnp.int32, (1, ghosts), 1)).astype(jnp.bfloat16)
        parts = jnp.stack([ghost_slot // 32, ghost_slot % 32], axis=1).astype(jnp.bfloat16)
        got = jnp.dot(pick, parts, preferred_element_type=jnp.float32)
        slot = (got[:, 0] * 32 + got[:, 1]).astype(jnp.int32)
        return jnp.where(index < NODE_DEV, index, NODE_DEV + slot)

    ends = column(edge_ends.reshape(-1)).reshape(2, -1)
    columns = lax.broadcasted_iota(jnp.int32, (1, width), 1)
    heads = ends[1][:, None] == columns
    tails = ends[0][:, None] == columns
    grad_matrix = lax.optimization_barrier(heads.astype(jnp.int8) - tails.astype(jnp.int8))
    nodes = lax.broadcasted_iota(jnp.int32, (NODE_DEV, 1), 0)
    owner_matrix = (nodes == owner_node[None, :]).astype(jnp.bfloat16)

    def gradient(owned):
        received = toward_ghosts(exact_dot(owned, owner_matrix, 0))
        table = jnp.concatenate([owned, received], axis=1)
        return exact_dot(table, grad_matrix, 1)

    def gather_owned(local):
        received = toward_owners(local[:, NODE_DEV:])
        return local[:, :NODE_DEV] + exact_dot(received, owner_matrix, 1)

    both = jnp.concatenate([modes_x, previous_p], axis=0)
    near = extend_field(both)
    stiff_both = apply_blocks(stiff_blocks, block_pattern, near)
    mass_both = apply_blocks(mass_blocks, block_pattern, near)
    stiff_x, stiff_p = stiff_both[:vectors], stiff_both[vectors:]
    mass_x, mass_p = mass_both[:vectors], mass_both[vectors:]
    both_faces = exchange_faces(jnp.concatenate([stiff_x, mass_x], axis=0))
    stiff_faces, mass_faces = both_faces[:vectors], both_faces[vectors:]
    upper, lower = jnp.split(
        all_sum(jnp.concatenate([jnp.sum(modes_x * stiff_x, axis=1), jnp.sum(modes_x * mass_x, axis=1)])), 2
    )
    ritz = upper / lower
    residual = stiff_x - ritz[:, None] * mass_x
    residual_faces = stiff_faces - ritz[:, None] * mass_faces
    mass_r = apply_blocks(mass_blocks, block_pattern, jnp.concatenate([residual, residual_faces], axis=1))

    rhs_local = exact_dot(mass_r, grad_matrix, 0)
    weight_local = exact_dot(lumped_mass[None], jnp.abs(grad_matrix), 0)
    owned_both = gather_owned(jnp.concatenate([rhs_local, weight_local], axis=0))
    rhs = owned_both[:vectors]
    diagonal = owned_both[vectors:]
    potential = OMEGA * rhs / diagonal
    for sweep in range(SWEEPS - 1):
        flux = lumped_mass[None] * gradient(potential)
        applied = gather_owned(exact_dot(flux, grad_matrix, 0))
        potential = potential + OMEGA * (rhs - applied) / diagonal
    projected = residual - gradient(potential)

    near_w = extend_field(projected)
    stiff_w = apply_blocks(stiff_blocks, block_pattern, near_w)
    mass_w = apply_blocks(mass_blocks, block_pattern, near_w)
    basis = jnp.concatenate([modes_x, projected, previous_p], axis=0)
    stiff_basis = jnp.concatenate([stiff_x, stiff_w, stiff_p], axis=0)
    mass_basis = jnp.concatenate([mass_x, mass_w, mass_p], axis=0)
    part_k = jnp.dot(basis, stiff_basis.T, precision=HIGH, preferred_element_type=jnp.float32)
    part_m = jnp.dot(basis, mass_basis.T, precision=HIGH, preferred_element_type=jnp.float32)
    summed_k, summed_m = all_sum(jnp.stack([part_k, part_m]))
    gram_k = 0.5 * (summed_k + summed_k.T)
    gram_m = 0.5 * (summed_m + summed_m.T)
    factor = jnp.linalg.cholesky(gram_m)
    left = jax.scipy.linalg.solve_triangular(factor, gram_k, lower=True)
    reduced = jax.scipy.linalg.solve_triangular(factor, left.T, lower=True)
    return (projected, reduced)


def solution(mesh):
    placed = (
        P(None, ("gx", "gy")),
        P(None, ("gx", "gy")),
        P(("gx", "gy"), None, None, None),
        P(("gx", "gy"), None, None, None),
        P(("gx", "gy"), None),
        P(("gx", "gy")),
        P(None, ("gx", "gy")),
        P(("gx", "gy")),
        P(("gx", "gy")),
    )
    return jax.shard_map(
        body, mesh=mesh, in_specs=placed, out_specs=(P(None, ("gx", "gy")), P()), check_vma=False
    )
```

```python
import jax
import jax.numpy as jnp
from jax import lax
from jax.sharding import PartitionSpec as P

BLOCK = 128
SWEEPS = 4
NODE_DEV = 1024
SLOTS = 256
TABLE = 1536


HIGH = lax.Precision.HIGHEST
OMEGA = 0.6


def from_behind(value, axis, steps):
    count = lax.axis_size(axis)
    received = lax.ppermute(value, axis, [(source, (source + steps) % count) for source in range(count)])
    place = lax.axis_index(axis) - steps
    return jnp.where((place >= 0) & (place < count), received, 0.0)


def all_sum(value):
    for axis in ("gx", "gy"):
        count = lax.axis_size(axis)
        if count & (count - 1):
            value = lax.psum(value, axis)
            continue
        step = 1
        while step < count:
            value = value + lax.ppermute(value, axis, [(i, i ^ step) for i in range(count)])
            step *= 2
    return value


def exchange_faces(field):
    length = field.shape[1]
    pieces = []
    for offset in (1, -1):
        face = field[:, length - BLOCK :] if offset == 1 else field[:, :BLOCK]
        pieces.append(from_behind(face, "gx", offset))
    for offset in (1, -1):
        face = (
            field[:, length - 2 * BLOCK : length - BLOCK]
            if offset == 1
            else field[:, BLOCK : 2 * BLOCK]
        )
        pieces.append(from_behind(face, "gy", offset))
    return jnp.concatenate(pieces, axis=1)


def extend_field(field):
    return jnp.concatenate([field, exchange_faces(field)], axis=1)


def apply_blocks(blocks, pattern, extended):
    vectors = extended.shape[0]
    tiles = extended.reshape(vectors, -1, BLOCK)
    picked = tiles[:, pattern]
    result = jnp.einsum("vrkj,rkij->vri", picked, blocks, precision=HIGH)
    return result.reshape(vectors, -1)


def split3(x):
    hi = lax.reduce_precision(x, exponent_bits=8, mantissa_bits=7)
    rest = x - hi
    mid = lax.reduce_precision(rest, exponent_bits=8, mantissa_bits=7)
    lo = rest - mid
    return jnp.concatenate([hi, mid, lo], axis=0).astype(jnp.bfloat16)


def exact_dot(x, matrix, contract):
    rows = x.shape[0]
    out = lax.dot_general(
        split3(x), matrix.astype(jnp.bfloat16), (((1,), (contract,)), ((), ())), preferred_element_type=jnp.float32
    )
    return (out[:rows] + out[rows : 2 * rows]) + out[2 * rows :]


def toward_owners(buffer):
    sections = []
    for direction in range(4):
        section = buffer[:, direction * SLOTS : (direction + 1) * SLOTS]
        if direction < 2:
            sections.append(from_behind(section, "gx", 2 * direction - 1))
        else:
            sections.append(from_behind(section, "gy", 2 * direction - 5))
    return jnp.concatenate(sections, axis=1)


def toward_ghosts(buffer):
    sections = []
    for direction in range(4):
        section = buffer[:, direction * SLOTS : (direction + 1) * SLOTS]
        if direction < 2:
            sections.append(from_behind(section, "gx", 1 - 2 * direction))
        else:
            sections.append(from_behind(section, "gy", 5 - 2 * direction))
    return jnp.concatenate(sections, axis=1)


def body(
    modes_x,
    previous_p,
    stiff_blocks,
    mass_blocks,
    block_pattern,
    lumped_mass,
    edge_ends,
    ghost_slot,
    owner_node,
):
    vectors = modes_x.shape[0]
    ghosts = ghost_slot.shape[0]
    slots = owner_node.shape[0]
    width = NODE_DEV + slots

    def column(index):
        ghost = index - NODE_DEV
        pick = (ghost[:, None] == lax.broadcasted_iota(jnp.int32, (1, ghosts), 1)).astype(jnp.bfloat16)
        parts = jnp.stack([ghost_slot // 32, ghost_slot % 32], axis=1).astype(jnp.bfloat16)
        got = jnp.dot(pick, parts, preferred_element_type=jnp.float32)
        slot = (got[:, 0] * 32 + got[:, 1]).astype(jnp.int32)
        return jnp.where(index < NODE_DEV, index, NODE_DEV + slot)

    ends = column(edge_ends.reshape(-1)).reshape(2, -1)
    columns = lax.broadcasted_iota(jnp.int32, (1, width), 1)
    heads = ends[1][:, None] == columns
    tails = ends[0][:, None] == columns
    grad_matrix = lax.optimization_barrier(heads.astype(jnp.bfloat16) - tails.astype(jnp.bfloat16))
    nodes = lax.broadcasted_iota(jnp.int32, (NODE_DEV, 1), 0)
    owner_matrix = (nodes == owner_node[None, :]).astype(jnp.bfloat16)

    def gradient(owned):
        received = toward_ghosts(exact_dot(owned, owner_matrix, 0))
        table = jnp.concatenate([owned, received], axis=1)
        return exact_dot(table, grad_matrix, 1)

    def gather_owned(local):
        received = toward_owners(local[:, NODE_DEV:])
        return local[:, :NODE_DEV] + exact_dot(received, owner_matrix, 1)

    both = jnp.concatenate([modes_x, previous_p], axis=0)
    near = extend_field(both)
    stiff_both = apply_blocks(stiff_blocks, block_pattern, near)
    mass_both = apply_blocks(mass_blocks, block_pattern, near)
    stiff_x, stiff_p = stiff_both[:vectors], stiff_both[vectors:]
    mass_x, mass_p = mass_both[:vectors], mass_both[vectors:]
    both_faces = exchange_faces(jnp.concatenate([stiff_x, mass_x], axis=0))
    stiff_faces, mass_faces = both_faces[:vectors], both_faces[vectors:]
    upper, lower = jnp.split(
        all_sum(jnp.concatenate([jnp.sum(modes_x * stiff_x, axis=1), jnp.sum(modes_x * mass_x, axis=1)])), 2
    )
    ritz = upper / lower
    residual = stiff_x - ritz[:, None] * mass_x
    residual_faces = stiff_faces - ritz[:, None] * mass_faces
    mass_r = apply_blocks(mass_blocks, block_pattern, jnp.concatenate([residual, residual_faces], axis=1))

    rhs_local = exact_dot(mass_r, grad_matrix, 0)
    weight_local = exact_dot(lumped_mass[None], jnp.abs(grad_matrix), 0)
    owned_both = gather_owned(jnp.concatenate([rhs_local, weight_local], axis=0))
    rhs = owned_both[:vectors]
    diagonal = owned_both[vectors:]
    potential = OMEGA * rhs / diagonal
    for sweep in range(SWEEPS - 1):
        flux = lumped_mass[None] * gradient(potential)
        applied = gather_owned(exact_dot(flux, grad_matrix, 0))
        potential = potential + OMEGA * (rhs - applied) / diagonal
    projected = residual - gradient(potential)

    near_w = extend_field(projected)
    stiff_w = apply_blocks(stiff_blocks, block_pattern, near_w)
    mass_w = apply_blocks(mass_blocks, block_pattern, near_w)
    basis = jnp.concatenate([modes_x, projected, previous_p], axis=0)
    stiff_basis = jnp.concatenate([stiff_x, stiff_w, stiff_p], axis=0)
    mass_basis = jnp.concatenate([mass_x, mass_w, mass_p], axis=0)
    part_k = jnp.dot(basis, stiff_basis.T, precision=HIGH, preferred_element_type=jnp.float32)
    part_m = jnp.dot(basis, mass_basis.T, precision=HIGH, preferred_element_type=jnp.float32)
    summed_k, summed_m = all_sum(jnp.stack([part_k, part_m]))
    gram_k = 0.5 * (summed_k + summed_k.T)
    gram_m = 0.5 * (summed_m + summed_m.T)
    factor = jnp.linalg.cholesky(gram_m)
    left = jax.scipy.linalg.solve_triangular(factor, gram_k, lower=True)
    reduced = jax.scipy.linalg.solve_triangular(factor, left.T, lower=True)
    return (projected, reduced)


def solution(mesh):
    placed = (
        P(None, ("gx", "gy")),
        P(None, ("gx", "gy")),
        P(("gx", "gy"), None, None, None),
        P(("gx", "gy"), None, None, None),
        P(("gx", "gy"), None),
        P(("gx", "gy")),
        P(None, ("gx", "gy")),
        P(("gx", "gy")),
        P(("gx", "gy")),
    )
    return jax.shard_map(
        body, mesh=mesh, in_specs=placed, out_specs=(P(None, ("gx", "gy")), P()), check_vma=False
    )
```

```python
import jax
import jax.numpy as jnp
from jax import lax
from jax.sharding import PartitionSpec as P

BLOCK = 128
SWEEPS = 4
NODE_DEV = 1024
SLOTS = 256
TABLE = 1536


HIGH = lax.Precision.HIGHEST
OMEGA = 0.6


def from_behind(value, axis, steps):
    count = lax.axis_size(axis)
    received = lax.ppermute(value, axis, [(source, (source + steps) % count) for source in range(count)])
    place = lax.axis_index(axis) - steps
    return jnp.where((place >= 0) & (place < count), received, 0.0)


def all_sum(value):
    for axis in ("gx", "gy"):
        count = lax.axis_size(axis)
        if count & (count - 1):
            value = lax.psum(value, axis)
            continue
        step = 1
        while step < count:
            value = value + lax.ppermute(value, axis, [(i, i ^ step) for i in range(count)])
            step *= 2
    return value


def exchange_faces(field):
    length = field.shape[1]
    pieces = []
    for offset in (1, -1):
        face = field[:, length - BLOCK :] if offset == 1 else field[:, :BLOCK]
        pieces.append(from_behind(face, "gx", offset))
    for offset in (1, -1):
        face = (
            field[:, length - 2 * BLOCK : length - BLOCK]
            if offset == 1
            else field[:, BLOCK : 2 * BLOCK]
        )
        pieces.append(from_behind(face, "gy", offset))
    return jnp.concatenate(pieces, axis=1)


def extend_field(field):
    return jnp.concatenate([field, exchange_faces(field)], axis=1)


def apply_blocks(blocks, pattern, extended):
    vectors = extended.shape[0]
    tiles = extended.reshape(vectors, -1, BLOCK)
    picked = tiles[:, pattern]
    result = jnp.einsum("vrkj,rkij->vri", picked, blocks, precision=HIGH)
    return result.reshape(vectors, -1)


def split3(x):
    hi = lax.reduce_precision(x, exponent_bits=8, mantissa_bits=7)
    rest = x - hi
    mid = lax.reduce_precision(rest, exponent_bits=8, mantissa_bits=7)
    lo = rest - mid
    return jnp.concatenate([hi, mid, lo], axis=0).astype(jnp.bfloat16)


def exact_dot(x, matrix, contract):
    rows = x.shape[0]
    out = lax.dot_general(
        split3(x), matrix.astype(jnp.bfloat16), (((1,), (contract,)), ((), ())), preferred_element_type=jnp.float32
    )
    return (out[:rows] + out[rows : 2 * rows]) + out[2 * rows :]


def toward_owners(buffer):
    sections = []
    for direction in range(4):
        section = buffer[:, direction * SLOTS : (direction + 1) * SLOTS]
        if direction < 2:
            sections.append(from_behind(section, "gx", 2 * direction - 1))
        else:
            sections.append(from_behind(section, "gy", 2 * direction - 5))
    return jnp.concatenate(sections, axis=1)


def toward_ghosts(buffer):
    sections = []
    for direction in range(4):
        section = buffer[:, direction * SLOTS : (direction + 1) * SLOTS]
        if direction < 2:
            sections.append(from_behind(section, "gx", 1 - 2 * direction))
        else:
            sections.append(from_behind(section, "gy", 5 - 2 * direction))
    return jnp.concatenate(sections, axis=1)


def body(
    modes_x,
    previous_p,
    stiff_blocks,
    mass_blocks,
    block_pattern,
    lumped_mass,
    edge_ends,
    ghost_slot,
    owner_node,
):
    vectors = modes_x.shape[0]
    ghosts = ghost_slot.shape[0]
    slots = owner_node.shape[0]
    width = NODE_DEV + slots

    def column(index):
        ghost = index - NODE_DEV
        pick = (ghost[:, None] == lax.broadcasted_iota(jnp.int32, (1, ghosts), 1)).astype(jnp.bfloat16)
        parts = jnp.stack([ghost_slot // 32, ghost_slot % 32], axis=1).astype(jnp.bfloat16)
        got = jnp.dot(pick, parts, preferred_element_type=jnp.float32)
        slot = (got[:, 0] * 32 + got[:, 1]).astype(jnp.int32)
        return jnp.where(index < NODE_DEV, index, NODE_DEV + slot)

    ends = column(edge_ends.reshape(-1)).reshape(2, -1)
    columns = lax.broadcasted_iota(jnp.int32, (1, width), 1)
    heads = ends[1][:, None] == columns
    tails = ends[0][:, None] == columns
    grad_matrix = lax.optimization_barrier(heads.astype(jnp.int8) - tails.astype(jnp.int8))
    nodes = lax.broadcasted_iota(jnp.int32, (NODE_DEV, 1), 0)
    owner_matrix = (nodes == owner_node[None, :]).astype(jnp.bfloat16)

    def gradient(owned):
        received = toward_ghosts(exact_dot(owned, owner_matrix, 0))
        table = jnp.concatenate([owned, received], axis=1)
        return exact_dot(table, grad_matrix, 1)

    def gather_owned(local):
        received = toward_owners(local[:, NODE_DEV:])
        return local[:, :NODE_DEV] + exact_dot(received, owner_matrix, 1)

    both = jnp.concatenate([modes_x, previous_p], axis=0)
    near = extend_field(both)
    stiff_both = apply_blocks(stiff_blocks, block_pattern, near)
    mass_both = apply_blocks(mass_blocks, block_pattern, near)
    stiff_x, stiff_p = stiff_both[:vectors], stiff_both[vectors:]
    mass_x, mass_p = mass_both[:vectors], mass_both[vectors:]
    both_faces = exchange_faces(jnp.concatenate([stiff_x, mass_x], axis=0))
    upper, lower = jnp.split(
        all_sum(jnp.concatenate([jnp.sum(modes_x * stiff_x, axis=1), jnp.sum(modes_x * mass_x, axis=1)])), 2
    )
    mass_km = apply_blocks(
        mass_blocks, block_pattern, jnp.concatenate([jnp.concatenate([stiff_x, mass_x], axis=0), both_faces], axis=1)
    )
    ritz = upper / lower
    residual = stiff_x - ritz[:, None] * mass_x
    mass_r = mass_km[:vectors] - ritz[:, None] * mass_km[vectors:]

    rhs_local = exact_dot(mass_r, grad_matrix, 0)
    weight_local = exact_dot(lumped_mass[None], jnp.abs(grad_matrix), 0)
    owned_both = gather_owned(jnp.concatenate([rhs_local, weight_local], axis=0))
    rhs = owned_both[:vectors]
    diagonal = owned_both[vectors:]
    potential = OMEGA * rhs / diagonal
    for sweep in range(SWEEPS - 1):
        flux = lumped_mass[None] * gradient(potential)
        applied = gather_owned(exact_dot(flux, grad_matrix, 0))
        potential = potential + OMEGA * (rhs - applied) / diagonal
    projected = residual - gradient(potential)

    near_w = extend_field(projected)
    stiff_w = apply_blocks(stiff_blocks, block_pattern, near_w)
    mass_w = apply_blocks(mass_blocks, block_pattern, near_w)
    basis = jnp.concatenate([modes_x, projected, previous_p], axis=0)
    stiff_basis = jnp.concatenate([stiff_x, stiff_w, stiff_p], axis=0)
    mass_basis = jnp.concatenate([mass_x, mass_w, mass_p], axis=0)
    part_k = jnp.dot(basis, stiff_basis.T, precision=HIGH, preferred_element_type=jnp.float32)
    part_m = jnp.dot(basis, mass_basis.T, precision=HIGH, preferred_element_type=jnp.float32)
    summed_k, summed_m = all_sum(jnp.stack([part_k, part_m]))
    gram_k = 0.5 * (summed_k + summed_k.T)
    gram_m = 0.5 * (summed_m + summed_m.T)
    factor = jnp.linalg.cholesky(gram_m)
    left = jax.scipy.linalg.solve_triangular(factor, gram_k, lower=True)
    reduced = jax.scipy.linalg.solve_triangular(factor, left.T, lower=True)
    return (projected, reduced)


def solution(mesh):
    placed = (
        P(None, ("gx", "gy")),
        P(None, ("gx", "gy")),
        P(("gx", "gy"), None, None, None),
        P(("gx", "gy"), None, None, None),
        P(("gx", "gy"), None),
        P(("gx", "gy")),
        P(None, ("gx", "gy")),
        P(("gx", "gy")),
        P(("gx", "gy")),
    )
    return jax.shard_map(
        body, mesh=mesh, in_specs=placed, out_specs=(P(None, ("gx", "gy")), P()), check_vma=False
    )
```

```python
import jax
import jax.numpy as jnp
from jax import lax
from jax.sharding import PartitionSpec as P

BLOCK = 128
SWEEPS = 4
NODE_DEV = 1024
SLOTS = 256
TABLE = 1536


HIGH = lax.Precision.HIGHEST
OMEGA = 0.6


def from_behind(value, axis, steps):
    count = lax.axis_size(axis)
    received = lax.ppermute(value, axis, [(source, (source + steps) % count) for source in range(count)])
    place = lax.axis_index(axis) - steps
    return jnp.where((place >= 0) & (place < count), received, 0.0)


def all_sum(value):
    for axis in ("gy", "gx"):
        count = lax.axis_size(axis)
        if count & (count - 1):
            value = lax.psum(value, axis)
            continue
        step = 1
        while step < count:
            value = value + lax.ppermute(value, axis, [(i, i ^ step) for i in range(count)])
            step *= 2
    return value


def exchange_faces(field):
    length = field.shape[1]
    pieces = []
    for offset in (1, -1):
        face = field[:, length - BLOCK :] if offset == 1 else field[:, :BLOCK]
        pieces.append(from_behind(face, "gx", offset))
    for offset in (1, -1):
        face = (
            field[:, length - 2 * BLOCK : length - BLOCK]
            if offset == 1
            else field[:, BLOCK : 2 * BLOCK]
        )
        pieces.append(from_behind(face, "gy", offset))
    return jnp.concatenate(pieces, axis=1)


def extend_field(field):
    return jnp.concatenate([field, exchange_faces(field)], axis=1)


def apply_blocks(blocks, pattern, extended):
    vectors = extended.shape[0]
    tiles = extended.reshape(vectors, -1, BLOCK)
    picked = tiles[:, pattern]
    result = jnp.einsum("vrkj,rkij->vri", picked, blocks, precision=HIGH)
    return result.reshape(vectors, -1)


def split3(x):
    hi = lax.reduce_precision(x, exponent_bits=8, mantissa_bits=7)
    rest = x - hi
    mid = lax.reduce_precision(rest, exponent_bits=8, mantissa_bits=7)
    lo = rest - mid
    return jnp.concatenate([hi, mid, lo], axis=0).astype(jnp.bfloat16)


def exact_dot(x, matrix, contract):
    rows = x.shape[0]
    out = lax.dot_general(
        split3(x), matrix.astype(jnp.bfloat16), (((1,), (contract,)), ((), ())), preferred_element_type=jnp.float32
    )
    return (out[:rows] + out[rows : 2 * rows]) + out[2 * rows :]


def toward_owners(buffer):
    sections = [None] * 4
    for direction in (2, 3, 0, 1):
        section = buffer[:, direction * SLOTS : (direction + 1) * SLOTS]
        if direction < 2:
            sections[direction] = from_behind(section, "gx", 2 * direction - 1)
        else:
            sections[direction] = from_behind(section, "gy", 2 * direction - 5)
    return jnp.concatenate(sections, axis=1)


def toward_ghosts(buffer):
    sections = [None] * 4
    for direction in (2, 3, 0, 1):
        section = buffer[:, direction * SLOTS : (direction + 1) * SLOTS]
        if direction < 2:
            sections[direction] = from_behind(section, "gx", 1 - 2 * direction)
        else:
            sections[direction] = from_behind(section, "gy", 5 - 2 * direction)
    return jnp.concatenate(sections, axis=1)


def body(
    modes_x,
    previous_p,
    stiff_blocks,
    mass_blocks,
    block_pattern,
    lumped_mass,
    edge_ends,
    ghost_slot,
    owner_node,
):
    vectors = modes_x.shape[0]
    ghosts = ghost_slot.shape[0]
    slots = owner_node.shape[0]
    width = NODE_DEV + slots

    def column(index):
        ghost = index - NODE_DEV
        pick = (ghost[:, None] == lax.broadcasted_iota(jnp.int32, (1, ghosts), 1)).astype(jnp.bfloat16)
        parts = jnp.stack([ghost_slot // 32, ghost_slot % 32], axis=1).astype(jnp.bfloat16)
        got = jnp.dot(pick, parts, preferred_element_type=jnp.float32)
        slot = (got[:, 0] * 32 + got[:, 1]).astype(jnp.int32)
        return jnp.where(index < NODE_DEV, index, NODE_DEV + slot)

    ends = column(edge_ends.reshape(-1)).reshape(2, -1)
    columns = lax.broadcasted_iota(jnp.int32, (1, width), 1)
    heads = ends[1][:, None] == columns
    tails = ends[0][:, None] == columns
    grad_matrix = lax.optimization_barrier(heads.astype(jnp.int8) - tails.astype(jnp.int8))
    nodes = lax.broadcasted_iota(jnp.int32, (NODE_DEV, 1), 0)
    owner_matrix = (nodes == owner_node[None, :]).astype(jnp.bfloat16)

    def gradient(owned):
        received = toward_ghosts(exact_dot(owned, owner_matrix, 0))
        table = jnp.concatenate([owned, received], axis=1)
        return exact_dot(table, grad_matrix, 1)

    def gather_owned(local):
        received = toward_owners(local[:, NODE_DEV:])
        return local[:, :NODE_DEV] + exact_dot(received, owner_matrix, 1)

    both = jnp.concatenate([modes_x, previous_p], axis=0)
    near = extend_field(both)
    stiff_both = apply_blocks(stiff_blocks, block_pattern, near)
    mass_both = apply_blocks(mass_blocks, block_pattern, near)
    stiff_x, stiff_p = stiff_both[:vectors], stiff_both[vectors:]
    mass_x, mass_p = mass_both[:vectors], mass_both[vectors:]
    both_faces = exchange_faces(jnp.concatenate([stiff_x, mass_x], axis=0))
    stiff_faces, mass_faces = both_faces[:vectors], both_faces[vectors:]
    upper, lower = jnp.split(
        all_sum(jnp.concatenate([jnp.sum(modes_x * stiff_x, axis=1), jnp.sum(modes_x * mass_x, axis=1)])), 2
    )
    ritz = upper / lower
    residual = stiff_x - ritz[:, None] * mass_x
    residual_faces = stiff_faces - ritz[:, None] * mass_faces
    mass_r = apply_blocks(mass_blocks, block_pattern, jnp.concatenate([residual, residual_faces], axis=1))

    rhs_local = exact_dot(mass_r, grad_matrix, 0)
    weight_local = exact_dot(lumped_mass[None], jnp.abs(grad_matrix), 0)
    owned_both = gather_owned(jnp.concatenate([rhs_local, weight_local], axis=0))
    rhs = owned_both[:vectors]
    diagonal = owned_both[vectors:]
    potential = OMEGA * rhs / diagonal
    for sweep in range(SWEEPS - 1):
        flux = lumped_mass[None] * gradient(potential)
        applied = gather_owned(exact_dot(flux, grad_matrix, 0))
        potential = potential + OMEGA * (rhs - applied) / diagonal
    projected = residual - gradient(potential)

    near_w = extend_field(projected)
    stiff_w = apply_blocks(stiff_blocks, block_pattern, near_w)
    mass_w = apply_blocks(mass_blocks, block_pattern, near_w)
    basis = jnp.concatenate([modes_x, projected, previous_p], axis=0)
    stiff_basis = jnp.concatenate([stiff_x, stiff_w, stiff_p], axis=0)
    mass_basis = jnp.concatenate([mass_x, mass_w, mass_p], axis=0)
    part_k = jnp.dot(basis, stiff_basis.T, precision=HIGH, preferred_element_type=jnp.float32)
    part_m = jnp.dot(basis, mass_basis.T, precision=HIGH, preferred_element_type=jnp.float32)
    summed_k, summed_m = all_sum(jnp.stack([part_k, part_m]))
    gram_k = 0.5 * (summed_k + summed_k.T)
    gram_m = 0.5 * (summed_m + summed_m.T)
    factor = jnp.linalg.cholesky(gram_m)
    left = jax.scipy.linalg.solve_triangular(factor, gram_k, lower=True)
    reduced = jax.scipy.linalg.solve_triangular(factor, left.T, lower=True)
    return (projected, reduced)


def solution(mesh):
    placed = (
        P(None, ("gx", "gy")),
        P(None, ("gx", "gy")),
        P(("gx", "gy"), None, None, None),
        P(("gx", "gy"), None, None, None),
        P(("gx", "gy"), None),
        P(("gx", "gy")),
        P(None, ("gx", "gy")),
        P(("gx", "gy")),
        P(("gx", "gy")),
    )
    return jax.shard_map(
        body, mesh=mesh, in_specs=placed, out_specs=(P(None, ("gx", "gy")), P()), check_vma=False
    )
```

```python
import jax
import jax.numpy as jnp
from jax import lax
from jax.sharding import PartitionSpec as P

BLOCK = 128
SWEEPS = 4
NODE_DEV = 1024
SLOTS = 256
TABLE = 1536


HIGH = lax.Precision.HIGHEST
OMEGA = 0.6


def from_behind(value, axis, steps):
    count = lax.axis_size(axis)
    received = lax.ppermute(value, axis, [(source, (source + steps) % count) for source in range(count)])
    place = lax.axis_index(axis) - steps
    return jnp.where((place >= 0) & (place < count), received, 0.0)


def all_sum(value):
    for axis in ("gy", "gx"):
        count = lax.axis_size(axis)
        if count & (count - 1):
            value = lax.psum(value, axis)
            continue
        step = 1
        while step < count:
            value = value + lax.ppermute(value, axis, [(i, i ^ step) for i in range(count)])
            step *= 2
    return value


def exchange_faces(field):
    length = field.shape[1]
    pieces = []
    for offset in (1, -1):
        face = field[:, length - BLOCK :] if offset == 1 else field[:, :BLOCK]
        pieces.append(from_behind(face, "gx", offset))
    for offset in (1, -1):
        face = (
            field[:, length - 2 * BLOCK : length - BLOCK]
            if offset == 1
            else field[:, BLOCK : 2 * BLOCK]
        )
        pieces.append(from_behind(face, "gy", offset))
    return jnp.concatenate(pieces, axis=1)


def extend_field(field):
    return jnp.concatenate([field, exchange_faces(field)], axis=1)


def apply_blocks(blocks, pattern, extended):
    vectors = extended.shape[0]
    tiles = extended.reshape(vectors, -1, BLOCK)
    picked = tiles[:, pattern]
    result = jnp.einsum("vrkj,rkij->vri", picked, blocks, precision=HIGH)
    return result.reshape(vectors, -1)


def split3(x):
    hi = lax.reduce_precision(x, exponent_bits=8, mantissa_bits=7)
    rest = x - hi
    mid = lax.reduce_precision(rest, exponent_bits=8, mantissa_bits=7)
    lo = rest - mid
    return jnp.concatenate([hi, mid, lo], axis=0).astype(jnp.bfloat16)


def exact_dot(x, matrix, contract):
    rows = x.shape[0]
    out = lax.dot_general(
        split3(x), matrix.astype(jnp.bfloat16), (((1,), (contract,)), ((), ())), preferred_element_type=jnp.float32
    )
    return (out[:rows] + out[rows : 2 * rows]) + out[2 * rows :]


def toward_owners(buffer):
    sections = [None] * 4
    for direction in (2, 3, 0, 1):
        section = buffer[:, direction * SLOTS : (direction + 1) * SLOTS]
        if direction < 2:
            sections[direction] = from_behind(section, "gx", 2 * direction - 1)
        else:
            sections[direction] = from_behind(section, "gy", 2 * direction - 5)
    return jnp.concatenate(sections, axis=1)


def toward_ghosts(buffer):
    sections = [None] * 4
    for direction in (2, 3, 0, 1):
        section = buffer[:, direction * SLOTS : (direction + 1) * SLOTS]
        if direction < 2:
            sections[direction] = from_behind(section, "gx", 1 - 2 * direction)
        else:
            sections[direction] = from_behind(section, "gy", 5 - 2 * direction)
    return jnp.concatenate(sections, axis=1)


def body(
    modes_x,
    previous_p,
    stiff_blocks,
    mass_blocks,
    block_pattern,
    lumped_mass,
    edge_ends,
    ghost_slot,
    owner_node,
):
    vectors = modes_x.shape[0]
    ghosts = ghost_slot.shape[0]
    slots = owner_node.shape[0]

    entries = lax.broadcasted_iota(jnp.int32, (1, NODE_DEV + ghosts), 1)
    heads = edge_ends[1][:, None] == entries
    tails = edge_ends[0][:, None] == entries
    grad_matrix = lax.optimization_barrier(heads.astype(jnp.int8) - tails.astype(jnp.int8))
    nodes = lax.broadcasted_iota(jnp.int32, (NODE_DEV, 1), 0)
    owner_matrix = (nodes == owner_node[None, :]).astype(jnp.bfloat16)
    slot_matrix = (ghost_slot[:, None] == lax.broadcasted_iota(jnp.int32, (1, slots), 1)).astype(jnp.bfloat16)

    def gradient(owned):
        received = toward_ghosts(exact_dot(owned, owner_matrix, 0))
        table = jnp.concatenate([owned, exact_dot(received, slot_matrix, 1)], axis=1)
        return exact_dot(table, grad_matrix, 1)

    def gather_owned(local):
        received = toward_owners(exact_dot(local[:, NODE_DEV:], slot_matrix, 0))
        return local[:, :NODE_DEV] + exact_dot(received, owner_matrix, 1)

    both = jnp.concatenate([modes_x, previous_p], axis=0)
    near = extend_field(both)
    stiff_both = apply_blocks(stiff_blocks, block_pattern, near)
    mass_both = apply_blocks(mass_blocks, block_pattern, near)
    stiff_x, stiff_p = stiff_both[:vectors], stiff_both[vectors:]
    mass_x, mass_p = mass_both[:vectors], mass_both[vectors:]
    both_faces = exchange_faces(jnp.concatenate([stiff_x, mass_x], axis=0))
    stiff_faces, mass_faces = both_faces[:vectors], both_faces[vectors:]
    upper, lower = jnp.split(
        all_sum(jnp.concatenate([jnp.sum(modes_x * stiff_x, axis=1), jnp.sum(modes_x * mass_x, axis=1)])), 2
    )
    ritz = upper / lower
    residual = stiff_x - ritz[:, None] * mass_x
    residual_faces = stiff_faces - ritz[:, None] * mass_faces
    mass_r = apply_blocks(mass_blocks, block_pattern, jnp.concatenate([residual, residual_faces], axis=1))

    rhs_local = exact_dot(mass_r, grad_matrix, 0)
    weight_local = exact_dot(lumped_mass[None], jnp.abs(grad_matrix), 0)
    owned_both = gather_owned(jnp.concatenate([rhs_local, weight_local], axis=0))
    rhs = owned_both[:vectors]
    diagonal = owned_both[vectors:]
    potential = OMEGA * rhs / diagonal
    for sweep in range(SWEEPS - 1):
        flux = lumped_mass[None] * gradient(potential)
        applied = gather_owned(exact_dot(flux, grad_matrix, 0))
        potential = potential + OMEGA * (rhs - applied) / diagonal
    projected = residual - gradient(potential)

    near_w = extend_field(projected)
    stiff_w = apply_blocks(stiff_blocks, block_pattern, near_w)
    mass_w = apply_blocks(mass_blocks, block_pattern, near_w)
    basis = jnp.concatenate([modes_x, projected, previous_p], axis=0)
    stiff_basis = jnp.concatenate([stiff_x, stiff_w, stiff_p], axis=0)
    mass_basis = jnp.concatenate([mass_x, mass_w, mass_p], axis=0)
    part_k = jnp.dot(basis, stiff_basis.T, precision=HIGH, preferred_element_type=jnp.float32)
    part_m = jnp.dot(basis, mass_basis.T, precision=HIGH, preferred_element_type=jnp.float32)
    summed_k, summed_m = all_sum(jnp.stack([part_k, part_m]))
    gram_k = 0.5 * (summed_k + summed_k.T)
    gram_m = 0.5 * (summed_m + summed_m.T)
    factor = jnp.linalg.cholesky(gram_m)
    left = jax.scipy.linalg.solve_triangular(factor, gram_k, lower=True)
    reduced = jax.scipy.linalg.solve_triangular(factor, left.T, lower=True)
    return (projected, reduced)


def solution(mesh):
    placed = (
        P(None, ("gx", "gy")),
        P(None, ("gx", "gy")),
        P(("gx", "gy"), None, None, None),
        P(("gx", "gy"), None, None, None),
        P(("gx", "gy"), None),
        P(("gx", "gy")),
        P(None, ("gx", "gy")),
        P(("gx", "gy")),
        P(("gx", "gy")),
    )
    return jax.shard_map(
        body, mesh=mesh, in_specs=placed, out_specs=(P(None, ("gx", "gy")), P()), check_vma=False
    )
```

```python
import jax
import jax.numpy as jnp
from jax import lax
from jax.sharding import PartitionSpec as P

BLOCK = 128
SWEEPS = 4
NODE_DEV = 1024
SLOTS = 256
TABLE = 1536


HIGH = lax.Precision.HIGHEST
OMEGA = 0.6


def from_behind(value, axis, steps):
    count = lax.axis_size(axis)
    received = lax.ppermute(value, axis, [(source, (source + steps) % count) for source in range(count)])
    place = lax.axis_index(axis) - steps
    return jnp.where((place >= 0) & (place < count), received, 0.0)


def all_sum(value):
    for axis in ("gy", "gx"):
        count = lax.axis_size(axis)
        if count & (count - 1):
            value = lax.psum(value, axis)
            continue
        step = 1
        while step < count:
            value = value + lax.ppermute(value, axis, [(i, i ^ step) for i in range(count)])
            step *= 2
    return value


def exchange_faces(field):
    length = field.shape[1]
    pieces = []
    for offset in (1, -1):
        face = field[:, length - BLOCK :] if offset == 1 else field[:, :BLOCK]
        pieces.append(from_behind(face, "gx", offset))
    for offset in (1, -1):
        face = (
            field[:, length - 2 * BLOCK : length - BLOCK]
            if offset == 1
            else field[:, BLOCK : 2 * BLOCK]
        )
        pieces.append(from_behind(face, "gy", offset))
    return jnp.concatenate(pieces, axis=1)


def extend_field(field):
    return jnp.concatenate([field, exchange_faces(field)], axis=1)


def apply_blocks(blocks, pattern, extended):
    vectors = extended.shape[0]
    tiles = extended.reshape(vectors, -1, BLOCK)
    picked = tiles[:, pattern]
    result = jnp.einsum("vrkj,rkij->vri", picked, blocks, precision=HIGH)
    return result.reshape(vectors, -1)


def split3(x):
    hi = lax.reduce_precision(x, exponent_bits=8, mantissa_bits=7)
    rest = x - hi
    mid = lax.reduce_precision(rest, exponent_bits=8, mantissa_bits=7)
    lo = rest - mid
    return jnp.concatenate([hi, mid, lo], axis=0).astype(jnp.bfloat16)


def exact_dot(x, matrix, contract):
    rows = x.shape[0]
    out = lax.dot_general(
        split3(x), matrix.astype(jnp.bfloat16), (((1,), (contract,)), ((), ())), preferred_element_type=jnp.float32
    )
    return (out[:rows] + out[rows : 2 * rows]) + out[2 * rows :]


def toward_owners(buffer):
    sections = [None] * 4
    for direction in (2, 3, 0, 1):
        section = buffer[:, direction * SLOTS : (direction + 1) * SLOTS]
        if direction < 2:
            sections[direction] = from_behind(section, "gx", 2 * direction - 1)
        else:
            sections[direction] = from_behind(section, "gy", 2 * direction - 5)
    return jnp.concatenate(sections, axis=1)


def toward_ghosts(buffer):
    sections = [None] * 4
    for direction in (2, 3, 0, 1):
        section = buffer[:, direction * SLOTS : (direction + 1) * SLOTS]
        if direction < 2:
            sections[direction] = from_behind(section, "gx", 1 - 2 * direction)
        else:
            sections[direction] = from_behind(section, "gy", 5 - 2 * direction)
    return jnp.concatenate(sections, axis=1)


def body(
    modes_x,
    previous_p,
    stiff_blocks,
    mass_blocks,
    block_pattern,
    lumped_mass,
    edge_ends,
    ghost_slot,
    owner_node,
):
    vectors = modes_x.shape[0]
    ghosts = ghost_slot.shape[0]
    slots = owner_node.shape[0]

    entries = lax.broadcasted_iota(jnp.int32, (1, NODE_DEV + ghosts), 1)
    heads = edge_ends[1][:, None] == entries
    tails = edge_ends[0][:, None] == entries
    grad_matrix = lax.optimization_barrier(heads.astype(jnp.int8) - tails.astype(jnp.int8))
    nodes = lax.broadcasted_iota(jnp.int32, (NODE_DEV, 1), 0)
    owner_matrix = (nodes == owner_node[None, :]).astype(jnp.bfloat16)
    slot_matrix = (ghost_slot[:, None] == lax.broadcasted_iota(jnp.int32, (1, slots), 1)).astype(jnp.bfloat16)

    def gradient(owned):
        received = toward_ghosts(exact_dot(owned, owner_matrix, 0))
        table = jnp.concatenate([owned, exact_dot(received, slot_matrix, 1)], axis=1)
        return exact_dot(table, grad_matrix, 1)

    def gather_owned(local):
        received = toward_owners(exact_dot(local[:, NODE_DEV:], slot_matrix, 0))
        return local[:, :NODE_DEV] + exact_dot(received, owner_matrix, 1)

    both = jnp.concatenate([modes_x, previous_p], axis=0)
    near = extend_field(both)
    stiff_both = apply_blocks(stiff_blocks, block_pattern, near)
    mass_both = apply_blocks(mass_blocks, block_pattern, near)
    stiff_x, stiff_p = stiff_both[:vectors], stiff_both[vectors:]
    mass_x, mass_p = mass_both[:vectors], mass_both[vectors:]
    both_faces = exchange_faces(jnp.concatenate([stiff_x, mass_x], axis=0))
    stiff_faces, mass_faces = both_faces[:vectors], both_faces[vectors:]
    upper, lower = jnp.split(
        all_sum(jnp.concatenate([jnp.sum(modes_x * stiff_x, axis=1), jnp.sum(modes_x * mass_x, axis=1)])), 2
    )
    ritz = upper / lower
    residual = stiff_x - ritz[:, None] * mass_x
    residual_faces = stiff_faces - ritz[:, None] * mass_faces
    mass_r = apply_blocks(mass_blocks, block_pattern, jnp.concatenate([residual, residual_faces], axis=1))

    rhs_local = exact_dot(mass_r, grad_matrix, 0)
    weight_local = exact_dot(lumped_mass[None], jnp.abs(grad_matrix), 0)
    owned_both = gather_owned(jnp.concatenate([rhs_local, weight_local], axis=0))
    rhs = owned_both[:vectors]
    diagonal = owned_both[vectors:]
    potential = OMEGA * rhs / diagonal
    def sweep(step, potential):
        flux = lumped_mass[None] * gradient(potential)
        applied = gather_owned(exact_dot(flux, grad_matrix, 0))
        return potential + OMEGA * (rhs - applied) / diagonal

    potential = lax.fori_loop(0, SWEEPS - 1, sweep, potential)
    projected = residual - gradient(potential)

    near_w = extend_field(projected)
    stiff_w = apply_blocks(stiff_blocks, block_pattern, near_w)
    mass_w = apply_blocks(mass_blocks, block_pattern, near_w)
    basis = jnp.concatenate([modes_x, projected, previous_p], axis=0)
    stiff_basis = jnp.concatenate([stiff_x, stiff_w, stiff_p], axis=0)
    mass_basis = jnp.concatenate([mass_x, mass_w, mass_p], axis=0)
    part_k = jnp.dot(basis, stiff_basis.T, precision=HIGH, preferred_element_type=jnp.float32)
    part_m = jnp.dot(basis, mass_basis.T, precision=HIGH, preferred_element_type=jnp.float32)
    summed_k, summed_m = all_sum(jnp.stack([part_k, part_m]))
    gram_k = 0.5 * (summed_k + summed_k.T)
    gram_m = 0.5 * (summed_m + summed_m.T)
    factor = jnp.linalg.cholesky(gram_m)
    left = jax.scipy.linalg.solve_triangular(factor, gram_k, lower=True)
    reduced = jax.scipy.linalg.solve_triangular(factor, left.T, lower=True)
    return (projected, reduced)


def solution(mesh):
    placed = (
        P(None, ("gx", "gy")),
        P(None, ("gx", "gy")),
        P(("gx", "gy"), None, None, None),
        P(("gx", "gy"), None, None, None),
        P(("gx", "gy"), None),
        P(("gx", "gy")),
        P(None, ("gx", "gy")),
        P(("gx", "gy")),
        P(("gx", "gy")),
    )
    return jax.shard_map(
        body, mesh=mesh, in_specs=placed, out_specs=(P(None, ("gx", "gy")), P()), check_vma=False
    )
```

```python
import jax
import jax.numpy as jnp
from jax import lax
from jax.sharding import PartitionSpec as P

BLOCK = 128
SWEEPS = 4
NODE_DEV = 1024
SLOTS = 256
TABLE = 1536


HIGH = lax.Precision.HIGHEST
OMEGA = 0.6


def from_behind(value, axis, steps):
    count = lax.axis_size(axis)
    received = lax.ppermute(value, axis, [(source, (source + steps) % count) for source in range(count)])
    place = lax.axis_index(axis) - steps
    return jnp.where((place >= 0) & (place < count), received, 0.0)


def all_sum(value):
    for axis in ("gy", "gx"):
        count = lax.axis_size(axis)
        if count & (count - 1):
            value = lax.psum(value, axis)
            continue
        step = 1
        while step < count:
            value = value + lax.ppermute(value, axis, [(i, i ^ step) for i in range(count)])
            step *= 2
    return value


def exchange_faces(field):
    length = field.shape[1]
    pieces = []
    for offset in (1, -1):
        face = field[:, length - BLOCK :] if offset == 1 else field[:, :BLOCK]
        pieces.append(from_behind(face, "gx", offset))
    for offset in (1, -1):
        face = (
            field[:, length - 2 * BLOCK : length - BLOCK]
            if offset == 1
            else field[:, BLOCK : 2 * BLOCK]
        )
        pieces.append(from_behind(face, "gy", offset))
    return jnp.concatenate(pieces, axis=1)


def extend_field(field):
    return jnp.concatenate([field, exchange_faces(field)], axis=1)


def apply_blocks(blocks, pattern, extended):
    vectors = extended.shape[0]
    tiles = extended.reshape(vectors, -1, BLOCK)
    picked = tiles[:, pattern]
    result = jnp.einsum("vrkj,rkij->vri", picked, blocks, precision=HIGH)
    return result.reshape(vectors, -1)


def split3(x):
    hi = lax.reduce_precision(x, exponent_bits=8, mantissa_bits=7)
    rest = x - hi
    mid = lax.reduce_precision(rest, exponent_bits=8, mantissa_bits=7)
    lo = rest - mid
    return jnp.concatenate([hi, mid, lo], axis=0).astype(jnp.bfloat16)


def exact_dot(x, matrix, contract):
    rows = x.shape[0]
    out = lax.dot_general(
        split3(x), matrix.astype(jnp.bfloat16), (((1,), (contract,)), ((), ())), preferred_element_type=jnp.float32
    )
    return (out[:rows] + out[rows : 2 * rows]) + out[2 * rows :]


def toward_owners(buffer):
    sections = [None] * 4
    for direction in (2, 3, 0, 1):
        section = buffer[:, direction * SLOTS : (direction + 1) * SLOTS]
        if direction < 2:
            sections[direction] = from_behind(section, "gx", 2 * direction - 1)
        else:
            sections[direction] = from_behind(section, "gy", 2 * direction - 5)
    return jnp.concatenate(sections, axis=1)


def toward_ghosts(buffer):
    sections = [None] * 4
    for direction in (2, 3, 0, 1):
        section = buffer[:, direction * SLOTS : (direction + 1) * SLOTS]
        if direction < 2:
            sections[direction] = from_behind(section, "gx", 1 - 2 * direction)
        else:
            sections[direction] = from_behind(section, "gy", 5 - 2 * direction)
    return jnp.concatenate(sections, axis=1)


def body(
    modes_x,
    previous_p,
    stiff_blocks,
    mass_blocks,
    block_pattern,
    lumped_mass,
    edge_ends,
    ghost_slot,
    owner_node,
):
    vectors = modes_x.shape[0]
    ghosts = ghost_slot.shape[0]
    slots = owner_node.shape[0]

    entries = lax.broadcasted_iota(jnp.int32, (NODE_DEV + ghosts, 1), 0)
    heads = entries == edge_ends[1][None, :]
    tails = entries == edge_ends[0][None, :]
    grad_matrix = lax.optimization_barrier(heads.astype(jnp.int8) - tails.astype(jnp.int8))
    nodes = lax.broadcasted_iota(jnp.int32, (NODE_DEV, 1), 0)
    owner_matrix = (nodes == owner_node[None, :]).astype(jnp.bfloat16)
    slot_matrix = (ghost_slot[:, None] == lax.broadcasted_iota(jnp.int32, (1, slots), 1)).astype(jnp.bfloat16)

    def gradient(owned):
        received = toward_ghosts(exact_dot(owned, owner_matrix, 0))
        table = jnp.concatenate([owned, exact_dot(received, slot_matrix, 1)], axis=1)
        return exact_dot(table, grad_matrix, 0)

    def gather_owned(local):
        received = toward_owners(exact_dot(local[:, NODE_DEV:], slot_matrix, 0))
        return local[:, :NODE_DEV] + exact_dot(received, owner_matrix, 1)

    both = jnp.concatenate([modes_x, previous_p], axis=0)
    near = extend_field(both)
    stiff_both = apply_blocks(stiff_blocks, block_pattern, near)
    mass_both = apply_blocks(mass_blocks, block_pattern, near)
    stiff_x, stiff_p = stiff_both[:vectors], stiff_both[vectors:]
    mass_x, mass_p = mass_both[:vectors], mass_both[vectors:]
    both_faces = exchange_faces(jnp.concatenate([stiff_x, mass_x], axis=0))
    stiff_faces, mass_faces = both_faces[:vectors], both_faces[vectors:]
    upper, lower = jnp.split(
        all_sum(jnp.concatenate([jnp.sum(modes_x * stiff_x, axis=1), jnp.sum(modes_x * mass_x, axis=1)])), 2
    )
    ritz = upper / lower
    residual = stiff_x - ritz[:, None] * mass_x
    residual_faces = stiff_faces - ritz[:, None] * mass_faces
    mass_r = apply_blocks(mass_blocks, block_pattern, jnp.concatenate([residual, residual_faces], axis=1))

    rhs_local = exact_dot(mass_r, grad_matrix, 1)
    weight_local = exact_dot(lumped_mass[None], jnp.abs(grad_matrix), 1)
    owned_both = gather_owned(jnp.concatenate([rhs_local, weight_local], axis=0))
    rhs = owned_both[:vectors]
    diagonal = owned_both[vectors:]
    potential = OMEGA * rhs / diagonal
    for sweep in range(SWEEPS - 1):
        flux = lumped_mass[None] * gradient(potential)
        applied = gather_owned(exact_dot(flux, grad_matrix, 1))
        potential = potential + OMEGA * (rhs - applied) / diagonal
    projected = residual - gradient(potential)

    near_w = extend_field(projected)
    stiff_w = apply_blocks(stiff_blocks, block_pattern, near_w)
    mass_w = apply_blocks(mass_blocks, block_pattern, near_w)
    basis = jnp.concatenate([modes_x, projected, previous_p], axis=0)
    stiff_basis = jnp.concatenate([stiff_x, stiff_w, stiff_p], axis=0)
    mass_basis = jnp.concatenate([mass_x, mass_w, mass_p], axis=0)
    part_k = jnp.dot(basis, stiff_basis.T, precision=HIGH, preferred_element_type=jnp.float32)
    part_m = jnp.dot(basis, mass_basis.T, precision=HIGH, preferred_element_type=jnp.float32)
    summed_k, summed_m = all_sum(jnp.stack([part_k, part_m]))
    gram_k = 0.5 * (summed_k + summed_k.T)
    gram_m = 0.5 * (summed_m + summed_m.T)
    factor = jnp.linalg.cholesky(gram_m)
    left = jax.scipy.linalg.solve_triangular(factor, gram_k, lower=True)
    reduced = jax.scipy.linalg.solve_triangular(factor, left.T, lower=True)
    return (projected, reduced)


def solution(mesh):
    placed = (
        P(None, ("gx", "gy")),
        P(None, ("gx", "gy")),
        P(("gx", "gy"), None, None, None),
        P(("gx", "gy"), None, None, None),
        P(("gx", "gy"), None),
        P(("gx", "gy")),
        P(None, ("gx", "gy")),
        P(("gx", "gy")),
        P(("gx", "gy")),
    )
    return jax.shard_map(
        body, mesh=mesh, in_specs=placed, out_specs=(P(None, ("gx", "gy")), P()), check_vma=False
    )
```

```python
import jax
import jax.numpy as jnp
from jax import lax
from jax.sharding import PartitionSpec as P

BLOCK = 128
SWEEPS = 4
NODE_DEV = 1024
SLOTS = 256
TABLE = 1536


HIGH = lax.Precision.HIGHEST
OMEGA = 0.6


def from_behind(value, axis, steps):
    count = lax.axis_size(axis)
    received = lax.ppermute(value, axis, [(source, (source + steps) % count) for source in range(count)])
    place = lax.axis_index(axis) - steps
    return jnp.where((place >= 0) & (place < count), received, 0.0)


def all_sum(value):
    for axis in ("gy", "gx"):
        count = lax.axis_size(axis)
        if count & (count - 1):
            value = lax.psum(value, axis)
            continue
        step = 1
        while step < count:
            value = value + lax.ppermute(value, axis, [(i, i ^ step) for i in range(count)])
            step *= 2
    return value


def exchange_faces(field):
    length = field.shape[1]
    pieces = []
    for offset in (1, -1):
        face = field[:, length - BLOCK :] if offset == 1 else field[:, :BLOCK]
        pieces.append(from_behind(face, "gx", offset))
    for offset in (1, -1):
        face = (
            field[:, length - 2 * BLOCK : length - BLOCK]
            if offset == 1
            else field[:, BLOCK : 2 * BLOCK]
        )
        pieces.append(from_behind(face, "gy", offset))
    return jnp.concatenate(pieces, axis=1)


def extend_field(field):
    return jnp.concatenate([field, exchange_faces(field)], axis=1)


def apply_blocks(blocks, pattern, extended):
    vectors = extended.shape[0]
    tiles = extended.reshape(vectors, -1, BLOCK)
    picked = tiles[:, pattern]
    result = jnp.einsum("vrkj,rkij->vri", picked, blocks, precision=HIGH)
    return result.reshape(vectors, -1)


def split3(x):
    hi = lax.reduce_precision(x, exponent_bits=8, mantissa_bits=7)
    rest = x - hi
    mid = lax.reduce_precision(rest, exponent_bits=8, mantissa_bits=7)
    lo = rest - mid
    return jnp.concatenate([hi, mid, lo], axis=0).astype(jnp.bfloat16)


def exact_dot(x, matrix, contract):
    rows = x.shape[0]
    out = lax.dot_general(
        split3(x), matrix.astype(jnp.bfloat16), (((1,), (contract,)), ((), ())), preferred_element_type=jnp.float32
    )
    return (out[:rows] + out[rows : 2 * rows]) + out[2 * rows :]


def toward_owners(buffer):
    sections = [None] * 4
    for direction in (2, 3, 0, 1):
        section = buffer[:, direction * SLOTS : (direction + 1) * SLOTS]
        if direction < 2:
            sections[direction] = from_behind(section, "gx", 2 * direction - 1)
        else:
            sections[direction] = from_behind(section, "gy", 2 * direction - 5)
    return jnp.concatenate(sections, axis=1)


def toward_ghosts(buffer):
    sections = [None] * 4
    for direction in (2, 3, 0, 1):
        section = buffer[:, direction * SLOTS : (direction + 1) * SLOTS]
        if direction < 2:
            sections[direction] = from_behind(section, "gx", 1 - 2 * direction)
        else:
            sections[direction] = from_behind(section, "gy", 5 - 2 * direction)
    return jnp.concatenate(sections, axis=1)


def body(
    modes_x,
    previous_p,
    stiff_blocks,
    mass_blocks,
    block_pattern,
    lumped_mass,
    edge_ends,
    ghost_slot,
    owner_node,
):
    vectors = modes_x.shape[0]
    ghosts = ghost_slot.shape[0]
    slots = owner_node.shape[0]

    entries = lax.broadcasted_iota(jnp.int32, (NODE_DEV + ghosts, 1), 0)
    heads = entries == edge_ends[1][None, :]
    tails = entries == edge_ends[0][None, :]
    grad_matrix = lax.optimization_barrier(heads.astype(jnp.int8) - tails.astype(jnp.int8))
    nodes = lax.broadcasted_iota(jnp.int32, (NODE_DEV, 1), 0)
    owner_matrix = (nodes == owner_node[None, :]).astype(jnp.bfloat16)
    slot_matrix = (ghost_slot[:, None] == lax.broadcasted_iota(jnp.int32, (1, slots), 1)).astype(jnp.bfloat16)

    def gradient(owned):
        received = toward_ghosts(exact_dot(owned, owner_matrix, 0))
        table = jnp.concatenate([owned, exact_dot(received, slot_matrix, 1)], axis=1)
        return exact_dot(table, grad_matrix, 0)

    def gather_owned(local):
        received = toward_owners(exact_dot(local[:, NODE_DEV:], slot_matrix, 0))
        return local[:, :NODE_DEV] + exact_dot(received, owner_matrix, 1)

    both = jnp.concatenate([modes_x, previous_p], axis=0)
    near = extend_field(both)
    stiff_both = apply_blocks(stiff_blocks, block_pattern, near)
    mass_both = apply_blocks(mass_blocks, block_pattern, near)
    stiff_x, stiff_p = stiff_both[:vectors], stiff_both[vectors:]
    mass_x, mass_p = mass_both[:vectors], mass_both[vectors:]
    both_faces = exchange_faces(jnp.concatenate([stiff_x, mass_x], axis=0))
    stiff_faces, mass_faces = both_faces[:vectors], both_faces[vectors:]
    upper, lower = jnp.split(
        all_sum(jnp.concatenate([jnp.sum(modes_x * stiff_x, axis=1), jnp.sum(modes_x * mass_x, axis=1)])), 2
    )
    ritz = upper / lower
    residual = stiff_x - ritz[:, None] * mass_x
    residual_faces = stiff_faces - ritz[:, None] * mass_faces
    mass_r = apply_blocks(mass_blocks, block_pattern, jnp.concatenate([residual, residual_faces], axis=1))

    rhs_local = exact_dot(mass_r, grad_matrix, 1)
    weight_local = exact_dot(lumped_mass[None], jnp.abs(grad_matrix), 1)
    owned_both = gather_owned(jnp.concatenate([rhs_local, weight_local], axis=0))
    rhs = owned_both[:vectors]
    diagonal = owned_both[vectors:]
    potential = OMEGA * rhs / diagonal
    for sweep in range(SWEEPS - 1):
        flux = lumped_mass[None] * gradient(potential)
        applied = gather_owned(exact_dot(flux, grad_matrix, 1))
        potential = potential + OMEGA * (rhs - applied) / diagonal
    projected = residual - gradient(potential)

    near_w = extend_field(projected)
    stiff_w = apply_blocks(stiff_blocks, block_pattern, near_w)
    mass_w = apply_blocks(mass_blocks, block_pattern, near_w)
    basis = jnp.concatenate([modes_x, projected, previous_p], axis=0)
    targets = jnp.concatenate([stiff_x, stiff_w, stiff_p, mass_x, mass_w, mass_p], axis=0)
    part = jnp.dot(basis, targets.T, precision=HIGH, preferred_element_type=jnp.float32)
    summed = all_sum(part)
    summed_k, summed_m = summed[:, : basis.shape[0]], summed[:, basis.shape[0] :]
    gram_k = 0.5 * (summed_k + summed_k.T)
    gram_m = 0.5 * (summed_m + summed_m.T)
    factor = jnp.linalg.cholesky(gram_m)
    left = jax.scipy.linalg.solve_triangular(factor, gram_k, lower=True)
    reduced = jax.scipy.linalg.solve_triangular(factor, left.T, lower=True)
    return (projected, reduced)


def solution(mesh):
    placed = (
        P(None, ("gx", "gy")),
        P(None, ("gx", "gy")),
        P(("gx", "gy"), None, None, None),
        P(("gx", "gy"), None, None, None),
        P(("gx", "gy"), None),
        P(("gx", "gy")),
        P(None, ("gx", "gy")),
        P(("gx", "gy")),
        P(("gx", "gy")),
    )
    return jax.shard_map(
        body, mesh=mesh, in_specs=placed, out_specs=(P(None, ("gx", "gy")), P()), check_vma=False
    )
```

```python
import jax
import jax.numpy as jnp
from jax import lax
from jax.sharding import PartitionSpec as P

BLOCK = 128
SWEEPS = 4
NODE_DEV = 1024
SLOTS = 256
TABLE = 1536


HIGH = lax.Precision.HIGHEST
OMEGA = 0.6


def from_behind(value, axis, steps):
    count = lax.axis_size(axis)
    received = lax.ppermute(value, axis, [(source, (source + steps) % count) for source in range(count)])
    place = lax.axis_index(axis) - steps
    return jnp.where((place >= 0) & (place < count), received, 0.0)


def all_sum(value):
    for axis in ("gy", "gx"):
        count = lax.axis_size(axis)
        if count & (count - 1):
            value = lax.psum(value, axis)
            continue
        step = 1
        while step < count:
            value = value + lax.ppermute(value, axis, [(i, i ^ step) for i in range(count)])
            step *= 2
    return value


def exchange_faces(field):
    length = field.shape[1]
    pieces = []
    for offset in (1, -1):
        face = field[:, length - BLOCK :] if offset == 1 else field[:, :BLOCK]
        pieces.append(from_behind(face, "gx", offset))
    for offset in (1, -1):
        face = (
            field[:, length - 2 * BLOCK : length - BLOCK]
            if offset == 1
            else field[:, BLOCK : 2 * BLOCK]
        )
        pieces.append(from_behind(face, "gy", offset))
    return jnp.concatenate(pieces, axis=1)


def extend_field(field):
    return jnp.concatenate([field, exchange_faces(field)], axis=1)


def apply_blocks(blocks, pattern, extended):
    vectors = extended.shape[0]
    tiles = extended.reshape(vectors, -1, BLOCK)
    picked = tiles[:, pattern]
    result = jnp.einsum("vrkj,rkij->vri", picked, blocks, precision=HIGH)
    return result.reshape(vectors, -1)


def split3(x):
    hi = lax.reduce_precision(x, exponent_bits=8, mantissa_bits=7)
    rest = x - hi
    mid = lax.reduce_precision(rest, exponent_bits=8, mantissa_bits=7)
    lo = rest - mid
    return jnp.concatenate([hi, mid, lo], axis=0).astype(jnp.bfloat16)


def exact_dot(x, matrix, contract):
    rows = x.shape[0]
    out = lax.dot_general(
        split3(x), matrix.astype(jnp.bfloat16), (((1,), (contract,)), ((), ())), preferred_element_type=jnp.float32
    )
    return (out[:rows] + out[rows : 2 * rows]) + out[2 * rows :]


def toward_owners(buffer):
    sections = [None] * 4
    for direction in (2, 3, 0, 1):
        section = buffer[:, direction * SLOTS : (direction + 1) * SLOTS]
        if direction < 2:
            sections[direction] = from_behind(section, "gx", 2 * direction - 1)
        else:
            sections[direction] = from_behind(section, "gy", 2 * direction - 5)
    return jnp.concatenate(sections, axis=1)


def toward_ghosts(buffer):
    sections = [None] * 4
    for direction in (2, 3, 0, 1):
        section = buffer[:, direction * SLOTS : (direction + 1) * SLOTS]
        if direction < 2:
            sections[direction] = from_behind(section, "gx", 1 - 2 * direction)
        else:
            sections[direction] = from_behind(section, "gy", 5 - 2 * direction)
    return jnp.concatenate(sections, axis=1)


def body(
    modes_x,
    previous_p,
    stiff_blocks,
    mass_blocks,
    block_pattern,
    lumped_mass,
    edge_ends,
    ghost_slot,
    owner_node,
):
    vectors = modes_x.shape[0]
    ghosts = ghost_slot.shape[0]
    slots = owner_node.shape[0]

    entries = lax.broadcasted_iota(jnp.int32, (NODE_DEV + ghosts, 1), 0)
    heads = entries == edge_ends[1][None, :]
    tails = entries == edge_ends[0][None, :]
    grad_matrix = lax.optimization_barrier(heads.astype(jnp.int8) - tails.astype(jnp.int8))
    nodes = lax.broadcasted_iota(jnp.int32, (NODE_DEV, 1), 0)
    owner_matrix = (nodes == owner_node[None, :]).astype(jnp.bfloat16)
    slot_matrix = (ghost_slot[:, None] == lax.broadcasted_iota(jnp.int32, (1, slots), 1)).astype(jnp.bfloat16)

    def gradient(owned):
        rows = owned.shape[0]
        pieces = split3(owned)
        picked = lax.dot_general(pieces, owner_matrix, (((1,), (0,)), ((), ())), preferred_element_type=jnp.float32)
        received = (toward_ghosts(picked) + 0.0 * lumped_mass[0]).astype(jnp.bfloat16)
        ghost_pieces = lax.dot_general(
            received, slot_matrix, (((1,), (1,)), ((), ())), preferred_element_type=jnp.float32
        ).astype(jnp.bfloat16)
        table = jnp.concatenate([pieces, ghost_pieces], axis=1)
        out = lax.dot_general(
            table, grad_matrix.astype(jnp.bfloat16), (((1,), (0,)), ((), ())), preferred_element_type=jnp.float32
        )
        return (out[:rows] + out[rows : 2 * rows]) + out[2 * rows :]

    def gather_owned(local):
        received = toward_owners(exact_dot(local[:, NODE_DEV:], slot_matrix, 0))
        return local[:, :NODE_DEV] + exact_dot(received, owner_matrix, 1)

    both = jnp.concatenate([modes_x, previous_p], axis=0)
    near = extend_field(both)
    stiff_both = apply_blocks(stiff_blocks, block_pattern, near)
    mass_both = apply_blocks(mass_blocks, block_pattern, near)
    stiff_x, stiff_p = stiff_both[:vectors], stiff_both[vectors:]
    mass_x, mass_p = mass_both[:vectors], mass_both[vectors:]
    both_faces = exchange_faces(jnp.concatenate([stiff_x, mass_x], axis=0))
    stiff_faces, mass_faces = both_faces[:vectors], both_faces[vectors:]
    upper, lower = jnp.split(
        all_sum(jnp.concatenate([jnp.sum(modes_x * stiff_x, axis=1), jnp.sum(modes_x * mass_x, axis=1)])), 2
    )
    ritz = upper / lower
    residual = stiff_x - ritz[:, None] * mass_x
    residual_faces = stiff_faces - ritz[:, None] * mass_faces
    mass_r = apply_blocks(mass_blocks, block_pattern, jnp.concatenate([residual, residual_faces], axis=1))

    rhs_local = exact_dot(mass_r, grad_matrix, 1)
    weight_local = exact_dot(lumped_mass[None], jnp.abs(grad_matrix), 1)
    owned_both = gather_owned(jnp.concatenate([rhs_local, weight_local], axis=0))
    rhs = owned_both[:vectors]
    diagonal = owned_both[vectors:]
    potential = OMEGA * rhs / diagonal
    for sweep in range(SWEEPS - 1):
        flux = lumped_mass[None] * gradient(potential)
        applied = gather_owned(exact_dot(flux, grad_matrix, 1))
        potential = potential + OMEGA * (rhs - applied) / diagonal
    projected = residual - gradient(potential)

    near_w = extend_field(projected)
    stiff_w = apply_blocks(stiff_blocks, block_pattern, near_w)
    mass_w = apply_blocks(mass_blocks, block_pattern, near_w)
    basis = jnp.concatenate([modes_x, projected, previous_p], axis=0)
    stiff_basis = jnp.concatenate([stiff_x, stiff_w, stiff_p], axis=0)
    mass_basis = jnp.concatenate([mass_x, mass_w, mass_p], axis=0)
    part_k = jnp.dot(basis, stiff_basis.T, precision=HIGH, preferred_element_type=jnp.float32)
    part_m = jnp.dot(basis, mass_basis.T, precision=HIGH, preferred_element_type=jnp.float32)
    summed_k, summed_m = all_sum(jnp.stack([part_k, part_m]))
    gram_k = 0.5 * (summed_k + summed_k.T)
    gram_m = 0.5 * (summed_m + summed_m.T)
    factor = jnp.linalg.cholesky(gram_m)
    left = jax.scipy.linalg.solve_triangular(factor, gram_k, lower=True)
    reduced = jax.scipy.linalg.solve_triangular(factor, left.T, lower=True)
    return (projected, reduced)


def solution(mesh):
    placed = (
        P(None, ("gx", "gy")),
        P(None, ("gx", "gy")),
        P(("gx", "gy"), None, None, None),
        P(("gx", "gy"), None, None, None),
        P(("gx", "gy"), None),
        P(("gx", "gy")),
        P(None, ("gx", "gy")),
        P(("gx", "gy")),
        P(("gx", "gy")),
    )
    return jax.shard_map(
        body, mesh=mesh, in_specs=placed, out_specs=(P(None, ("gx", "gy")), P()), check_vma=False
    )
```

```python
import jax
import jax.numpy as jnp
from jax import lax
from jax.sharding import PartitionSpec as P

BLOCK = 128
SWEEPS = 4
NODE_DEV = 1024
SLOTS = 256
TABLE = 1536


HIGH = lax.Precision.HIGHEST
OMEGA = 0.6


def from_behind(value, axis, steps):
    count = lax.axis_size(axis)
    received = lax.ppermute(value, axis, [(source, (source + steps) % count) for source in range(count)])
    place = lax.axis_index(axis) - steps
    return jnp.where((place >= 0) & (place < count), received, 0.0)


def all_sum(value):
    for axis in ("gy", "gx"):
        count = lax.axis_size(axis)
        if count & (count - 1):
            value = lax.psum(value, axis)
            continue
        step = 1
        while step < count:
            value = value + lax.ppermute(value, axis, [(i, i ^ step) for i in range(count)])
            step *= 2
    return value


def exchange_faces(field):
    length = field.shape[1]
    pieces = []
    for offset in (1, -1):
        face = field[:, length - BLOCK :] if offset == 1 else field[:, :BLOCK]
        pieces.append(from_behind(face, "gx", offset))
    for offset in (1, -1):
        face = (
            field[:, length - 2 * BLOCK : length - BLOCK]
            if offset == 1
            else field[:, BLOCK : 2 * BLOCK]
        )
        pieces.append(from_behind(face, "gy", offset))
    return jnp.concatenate(pieces, axis=1)


def extend_field(field):
    return jnp.concatenate([field, exchange_faces(field)], axis=1)


def apply_blocks(blocks, pattern, extended):
    vectors = extended.shape[0]
    tiles = extended.reshape(vectors, -1, BLOCK)
    picked = tiles[:, pattern]
    result = jnp.einsum("vrkj,rkij->vri", picked, blocks, precision=HIGH)
    return result.reshape(vectors, -1)


def split3(x):
    hi = lax.reduce_precision(x, exponent_bits=8, mantissa_bits=7)
    rest = x - hi
    mid = lax.reduce_precision(rest, exponent_bits=8, mantissa_bits=7)
    lo = rest - mid
    return jnp.concatenate([hi, mid, lo], axis=0).astype(jnp.bfloat16)


def exact_dot(x, matrix, contract):
    rows = x.shape[0]
    out = lax.dot_general(
        split3(x), matrix.astype(jnp.bfloat16), (((1,), (contract,)), ((), ())), preferred_element_type=jnp.float32
    )
    return (out[:rows] + out[rows : 2 * rows]) + out[2 * rows :]


def toward_owners(buffer):
    sections = [None] * 4
    for direction in (2, 3, 0, 1):
        section = buffer[:, direction * SLOTS : (direction + 1) * SLOTS]
        if direction < 2:
            sections[direction] = from_behind(section, "gx", 2 * direction - 1)
        else:
            sections[direction] = from_behind(section, "gy", 2 * direction - 5)
    return jnp.concatenate(sections, axis=1)


def toward_ghosts(buffer):
    sections = [None] * 4
    for direction in (2, 3, 0, 1):
        section = buffer[:, direction * SLOTS : (direction + 1) * SLOTS]
        if direction < 2:
            sections[direction] = from_behind(section, "gx", 1 - 2 * direction)
        else:
            sections[direction] = from_behind(section, "gy", 5 - 2 * direction)
    return jnp.concatenate(sections, axis=1)


def body(
    modes_x,
    previous_p,
    stiff_blocks,
    mass_blocks,
    block_pattern,
    lumped_mass,
    edge_ends,
    ghost_slot,
    owner_node,
):
    vectors = modes_x.shape[0]
    ghosts = ghost_slot.shape[0]
    slots = owner_node.shape[0]

    entries = lax.broadcasted_iota(jnp.int32, (NODE_DEV + ghosts, 1), 0)
    heads = entries == edge_ends[1][None, :]
    tails = entries == edge_ends[0][None, :]
    grad_matrix = lax.optimization_barrier(heads.astype(jnp.int8) - tails.astype(jnp.int8))
    nodes = lax.broadcasted_iota(jnp.int32, (NODE_DEV, 1), 0)
    owner_matrix = (nodes == owner_node[None, :]).astype(jnp.bfloat16)
    slot_matrix = (ghost_slot[:, None] == lax.broadcasted_iota(jnp.int32, (1, slots), 1)).astype(jnp.bfloat16)

    def gradient(owned):
        received = toward_ghosts(exact_dot(owned, owner_matrix, 0))
        table = jnp.concatenate([owned, exact_dot(received, slot_matrix, 1)], axis=1)
        return exact_dot(table, grad_matrix, 0)

    def gather_owned(local):
        received = toward_owners(exact_dot(local[:, NODE_DEV:], slot_matrix, 0))
        return local[:, :NODE_DEV] + exact_dot(received, owner_matrix, 1)

    both = jnp.concatenate([modes_x, previous_p], axis=0)
    near = extend_field(both)
    stiff_both = apply_blocks(stiff_blocks, block_pattern, near)
    mass_both = apply_blocks(mass_blocks, block_pattern, near)
    stiff_x, stiff_p = stiff_both[:vectors], stiff_both[vectors:]
    mass_x, mass_p = mass_both[:vectors], mass_both[vectors:]
    both_faces = exchange_faces(jnp.concatenate([stiff_x, mass_x], axis=0))
    stiff_faces, mass_faces = both_faces[:vectors], both_faces[vectors:]
    upper, lower = jnp.split(
        all_sum(jnp.concatenate([jnp.sum(modes_x * stiff_x, axis=1), jnp.sum(modes_x * mass_x, axis=1)])), 2
    )
    ritz = upper / lower
    residual = stiff_x - ritz[:, None] * mass_x
    residual_faces = stiff_faces - ritz[:, None] * mass_faces
    mass_r = apply_blocks(mass_blocks, block_pattern, jnp.concatenate([residual, residual_faces], axis=1))

    rhs_local = exact_dot(mass_r, grad_matrix, 1)
    touch = (jnp.abs(entries - edge_ends[1][None, :]) == 0) | (jnp.abs(entries - edge_ends[0][None, :]) == 0)
    weight_local = exact_dot(lumped_mass[None], touch.astype(jnp.bfloat16), 1)
    owned_both = gather_owned(jnp.concatenate([rhs_local, weight_local], axis=0))
    rhs = owned_both[:vectors]
    diagonal = owned_both[vectors:]
    potential = OMEGA * rhs / diagonal
    for sweep in range(SWEEPS - 1):
        flux = lumped_mass[None] * gradient(potential)
        applied = gather_owned(exact_dot(flux, grad_matrix, 1))
        potential = potential + OMEGA * (rhs - applied) / diagonal
    projected = residual - gradient(potential)

    near_w = extend_field(projected)
    stiff_w = apply_blocks(stiff_blocks, block_pattern, near_w)
    mass_w = apply_blocks(mass_blocks, block_pattern, near_w)
    basis = jnp.concatenate([modes_x, projected, previous_p], axis=0)
    stiff_basis = jnp.concatenate([stiff_x, stiff_w, stiff_p], axis=0)
    mass_basis = jnp.concatenate([mass_x, mass_w, mass_p], axis=0)
    part_k = jnp.dot(basis, stiff_basis.T, precision=HIGH, preferred_element_type=jnp.float32)
    part_m = jnp.dot(basis, mass_basis.T, precision=HIGH, preferred_element_type=jnp.float32)
    summed_k, summed_m = all_sum(jnp.stack([part_k, part_m]))
    gram_k = 0.5 * (summed_k + summed_k.T)
    gram_m = 0.5 * (summed_m + summed_m.T)
    factor = jnp.linalg.cholesky(gram_m)
    left = jax.scipy.linalg.solve_triangular(factor, gram_k, lower=True)
    reduced = jax.scipy.linalg.solve_triangular(factor, left.T, lower=True)
    return (projected, reduced)


def solution(mesh):
    placed = (
        P(None, ("gx", "gy")),
        P(None, ("gx", "gy")),
        P(("gx", "gy"), None, None, None),
        P(("gx", "gy"), None, None, None),
        P(("gx", "gy"), None),
        P(("gx", "gy")),
        P(None, ("gx", "gy")),
        P(("gx", "gy")),
        P(("gx", "gy")),
    )
    return jax.shard_map(
        body, mesh=mesh, in_specs=placed, out_specs=(P(None, ("gx", "gy")), P()), check_vma=False
    )
```
